32 devices in a mesh: groups: 2 (over x), wide: 16 (over z, y, core).
Axes of the slice: x: 2, y: 2, z: 4, core: 2. Of those that a mesh axis runs over, the one named last changes fastest.
Arguments:
- query_act: bfloat16 [4096, 2048], P(('groups', 'wide')), parts along dimension 0, may hold values from -6 to 6
- query_grad: bfloat16 [4096, 4096], P(('groups', 'wide')), parts along dimension 0, may hold values from -6 to 6
- query_positions: int32 [4096], P(('groups', 'wide')), parts along dimension 0, may hold values from 0 to 4095
- act_basis: bfloat16 [2048, 1024], P(None, 'wide'), may hold values from -0.125 to 0.125
- grad_basis: bfloat16 [4096, 2048], P(None, 'wide'), may hold values from -0.09375 to 0.09375
- eig_values: bfloat16 [1024, 2048], P('wide'), may hold values from 0.05 to 50, as said below
- damping_index: int32 [12], P('groups'), parts along dimension 0, may hold values from 0 to 8
- train_act_rot: bfloat16 [1024, 6144], P(None, 'wide'), may hold values from -6 to 6
- train_grad_rot: bfloat16 [2048, 6144], P(None, 'wide'), may hold values from -6 to 6
- train_positions: int32 [6144], P('wide'), may hold values from 0 to 4095
Outputs:
- influences: float32 [12, 6144], P('groups', 'wide'), parts along dimension 0
The draws below stay inside these ranges and needn't reach their ends.
There are 2 independent parts, one for each index of `groups`. The reference program is written for one: setup_inputs(seed, part) draws one part's arguments, and reference() takes and returns one part's arrays. A program takes and returns all parts, laid end to end along the dimension named above; an argument that names none is the same for every part. Nothing has to cross between parts.
Inputs may be any that keep to these rules, and one draw needn't show every extreme that they name: `eig_values`: positive corrected eigenvalues.
All inputs are finite; a program needn't handle non-finite values.
Results may differ from the reference program's by a relative error of at most 0.0059.
Values may be sent and summed in bfloat16 or wider, within the bound.
No kernel may reach another device: no remote copies, remote signals or barrier semaphores. Data moves between devices by JAX's collectives and lax.ppermute only.
A program may use at most 128 MiB of HBM per device.

```python
import math
import jax
import jax.numpy as jnp
from jax import lax

D_IN = 2048
D_OUT = 4096
EIG_IN = 1024
EIG_OUT = 2048
NDAMP = 6
SEQ = 4096
PROMPT = 1024
QTOKENS = 2048
TRAIN = 6144


def draw_eig_values(key, part):
    first, second, third = jax.random.split(key, 3)
    rising = jnp.exp(math.log(3.0) * jnp.arange(EIG_IN, dtype=jnp.float32) / EIG_IN)
    row_scale = jnp.exp(jax.random.uniform(first, (EIG_IN, 1), jnp.float32, 0.0, math.log(10.0))) * rising[:, None]
    col_scale = jnp.exp(jax.random.uniform(second, (1, EIG_OUT), jnp.float32, 0.0, math.log(10.0)))
    rough = jnp.exp(jax.random.uniform(third, (EIG_IN, EIG_OUT), jnp.float32, -0.5, 0.5))
    return (0.1 * row_scale * col_scale * rough).astype(jnp.bfloat16)


def set_ends(entries, rng, smallest, high):
    extent = entries.shape
    spot = [jax.random.randint(jax.random.fold_in(rng, axis), (), 0, extent[axis]) for axis in range(len(extent))]
    entries = entries.at[tuple(spot)].set(smallest)
    longest = extent.index(max(extent))
    spot[longest] = (spot[longest] + 1) % extent[longest]
    return entries.at[tuple(spot)].set(high)


def steps_of(key, extent, cuts, low, high):
    def one(dim, parts):
        steps = jax.random.uniform(jax.random.fold_in(jax.random.fold_in(key, 6), dim), (parts,), jnp.float32, low / len(cuts), high / len(cuts))
        return jnp.repeat(jnp.exp(steps), extent[dim] // parts).reshape((-1,) + (1,) * (len(extent) - dim - 1))

    factor_of = one(*cuts[0])
    for cut in cuts[1:]:
        factor_of = factor_of * one(*cut)
    return factor_of


def centred(key, extent, deviation, most, pieces=(), kind=jnp.bfloat16):
    drawn = jax.random.normal(key, extent, jnp.float32) * deviation
    if len(pieces) > 0:
        drawn = steps_of(key, extent, pieces, -0.22, 0.18) * drawn
    return jnp.clip(drawn, min=-most, max=most).astype(kind)


def setup_inputs(seed: int = 0, part: int = 0) -> dict:
    streams_of = jax.random.split(jax.random.key(seed), 11)
    part_splits = jax.random.split(jax.random.fold_in(streams_of[10], part), 11)
    query_act = centred(part_splits[0], (QTOKENS, D_IN), 1.0, 6.0, ((0, 16),))
    query_grad = centred(part_splits[1], (QTOKENS, D_OUT), 1.0, 6.0, ((0, 16),))
    query_positions = set_ends(jax.random.randint(part_splits[2], (QTOKENS,), 0, SEQ), jax.random.fold_in(part_splits[2], 1), 0, SEQ - 1).astype(jnp.int32)
    act_basis = centred(streams_of[3], (D_IN, EIG_IN), D_IN ** -0.5, 0.125, ((1, 16),))
    grad_basis = centred(streams_of[4], (D_OUT, EIG_OUT), D_OUT ** -0.5, 0.09375, ((1, 16),))
    eig_values = draw_eig_values(jax.random.fold_in(streams_of[10], 71), part)
    damping_index = set_ends(jax.random.randint(part_splits[6], (NDAMP,), 0, 9), jax.random.fold_in(part_splits[6], 1), 0, 8).astype(jnp.int32)
    train_act_rot = centred(streams_of[7], (EIG_IN, TRAIN), 1.0, 6.0, ((1, 16),))
    train_grad_rot = centred(streams_of[8], (EIG_OUT, TRAIN), 1.0, 6.0, ((1, 16),))
    train_positions = set_ends(jax.random.randint(streams_of[9], (TRAIN,), 0, SEQ), jax.random.fold_in(streams_of[9], 1), 0, SEQ - 1).astype(jnp.int32)
    return {"query_act": query_act, "query_grad": query_grad, "query_positions": query_positions, "act_basis": act_basis, "grad_basis": grad_basis, "eig_values": eig_values, "damping_index": damping_index, "train_act_rot": train_act_rot, "train_grad_rot": train_grad_rot, "train_positions": train_positions}


def rotate_side(rows, basis):
    return jnp.dot(rows, basis, preferred_element_type=jnp.float32).astype(jnp.bfloat16)

def reference(query_act, query_grad, query_positions, act_basis, grad_basis, eig_values, damping_index, train_act_rot, train_grad_rot, train_positions):
    act_rot = rotate_side(query_act, act_basis)
    grad_rot = rotate_side(query_grad, grad_basis)
    query_weight = jnp.where(query_positions >= PROMPT, 1.0, 0.0).astype(jnp.bfloat16)
    grad_kept = grad_rot * query_weight[:, None]
    query_gradient = lax.dot_general(act_rot, grad_kept, (((0,), (0,)), ((), ())), preferred_element_type=jnp.float32).astype(jnp.bfloat16)
    eig_wide = eig_values.astype(jnp.float32)
    mean_eig = jnp.sum(eig_wide) / (EIG_IN * EIG_OUT)
    dampings = mean_eig * jnp.exp2(damping_index.astype(jnp.float32) - 4.0)
    acts_wide = train_act_rot.astype(jnp.float32)

    def score(damping):
        precond = (query_gradient.astype(jnp.float32) / (eig_wide + damping)).astype(jnp.bfloat16)
        projected = jnp.dot(precond, train_grad_rot, preferred_element_type=jnp.float32)
        return lax.optimization_barrier(jnp.sum(acts_wide * projected, axis=0))
    totals = lax.map(score, dampings)
    train_weight = jnp.where(train_positions >= PROMPT, 1.0, 0.0).astype(jnp.float32)
    factor = mean_eig * (1.0 / math.sqrt(float(QTOKENS) * EIG_IN * EIG_OUT))
    return totals * factor * train_weight[None, :]
```

```python
import math

import jax
import jax.numpy as jnp
from jax import lax
from jax.sharding import Mesh
from jax.sharding import PartitionSpec as P

PROMPT = 1024
WIDE = ("wa", "wb")


def score_rows(grad_rows, eig_rows, dampings, train_act_rot, train_grad_rot):
    acts_rows = train_act_rot.astype(jnp.float32)
    grad_wide = grad_rows.astype(jnp.float32)
    eig_wide = eig_rows.astype(jnp.float32)
    results = []
    for damping in range(dampings.shape[0]):
        precond = (grad_wide / (eig_wide + dampings[damping])).astype(jnp.bfloat16)
        projected = jnp.dot(precond, train_grad_rot, preferred_element_type=jnp.float32)
        results.append(jnp.sum(projected * acts_rows, axis=0))
    return jnp.stack(results)


def shards(
    query_act,
    query_grad,
    query_positions,
    act_basis,
    grad_basis,
    eig_values,
    damping_index,
    train_act_rot,
    train_grad_rot,
    train_positions,
):
    act_tokens = lax.all_gather(query_act, "wa", axis=0, tiled=True)
    grad_tokens = lax.all_gather(query_grad, "wa", axis=0, tiled=True)
    positions = lax.all_gather(query_positions, "wa", axis=0, tiled=True)
    act_cols = lax.all_gather(act_basis, "wb", axis=1, tiled=True)
    grad_cols = lax.all_gather(grad_basis, "wb", axis=1, tiled=True)
    act_rot = jnp.dot(act_tokens, act_cols, preferred_element_type=jnp.float32).astype(jnp.bfloat16)
    grad_rot = jnp.dot(grad_tokens, grad_cols, preferred_element_type=jnp.float32).astype(jnp.bfloat16)
    query_weight = jnp.where(positions >= PROMPT, 1.0, 0.0).astype(jnp.bfloat16)
    grad_kept = grad_rot * query_weight[:, None]
    grad_all = lax.all_gather(grad_kept, "wa", axis=1, tiled=True)
    partial_rows = lax.dot_general(
        act_rot, grad_all, (((0,), (0,)), ((), ())), preferred_element_type=jnp.float32
    )
    gradient_rows = lax.psum_scatter(partial_rows, "wb", scatter_dimension=0, tiled=True)
    query_gradient = lax.all_gather(gradient_rows.astype(jnp.bfloat16), WIDE, axis=0, tiled=True)
    eig_full = lax.all_gather(eig_values, WIDE, axis=0, tiled=True)
    eig_in, eig_out = eig_full.shape
    mean_eig = jnp.sum(eig_full.astype(jnp.float32)) / (eig_in * eig_out)
    dampings = mean_eig * jnp.exp2(damping_index.astype(jnp.float32) - 4.0)
    totals = score_rows(query_gradient, eig_full, dampings, train_act_rot, train_grad_rot)
    query_count = query_act.shape[0] * lax.axis_size(WIDE)
    factor = mean_eig * (1.0 / math.sqrt(float(query_count) * eig_in * eig_out))
    train_weight = jnp.where(train_positions >= PROMPT, 1.0, 0.0).astype(jnp.float32)
    return totals * factor * train_weight[None, :]


def split_wide(size):
    wb = 1
    while wb * wb < size and size % (wb * 2) == 0:
        wb *= 2
    return size // wb, wb


def solution(mesh):
    groups, wide = mesh.devices.shape
    wa, wb = split_wide(wide)
    grid = Mesh(mesh.devices.reshape(groups, wa, wb), ("groups",) + WIDE)
    tokens = ("groups",) + WIDE
    in_specs = (
        P(tokens, None),
        P(tokens, None),
        P(tokens),
        P(None, WIDE),
        P(None, WIDE),
        P(WIDE, None),
        P("groups"),
        P(None, WIDE),
        P(None, WIDE),
        P(WIDE),
    )
    out_specs = P("groups", WIDE)
    return jax.shard_map(shards, mesh=grid, in_specs=in_specs, out_specs=out_specs, check_vma=False)
```

```python
import math

import jax
import jax.numpy as jnp
from jax import lax
from jax.sharding import Mesh
from jax.sharding import PartitionSpec as P

PROMPT = 1024
WIDE = ("wa", "wb")


def score_rows(grad_rows, eig_rows, dampings, train_act_rot, train_grad_rot):
    acts_rows = train_act_rot.astype(jnp.float32)
    grad_wide = grad_rows.astype(jnp.float32)
    eig_wide = eig_rows.astype(jnp.float32)
    results = []
    for damping in range(dampings.shape[0]):
        precond = (grad_wide / (eig_wide + dampings[damping])).astype(jnp.bfloat16)
        projected = jnp.dot(precond, train_grad_rot, preferred_element_type=jnp.float32)
        results.append(jnp.sum(projected * acts_rows, axis=0))
    return jnp.stack(results)


def shards(
    query_act,
    query_grad,
    query_positions,
    act_basis,
    grad_basis,
    eig_values,
    damping_index,
    train_act_rot,
    train_grad_rot,
    train_positions,
):
    act_tokens = lax.all_gather(query_act, "wb", axis=0, tiled=True)
    grad_tokens = lax.all_gather(query_grad, "wb", axis=0, tiled=True)
    positions = lax.all_gather(query_positions, "wb", axis=0, tiled=True)
    act_cols = lax.all_gather(act_basis, "wa", axis=1, tiled=True)
    grad_cols = lax.all_gather(grad_basis, "wa", axis=1, tiled=True)
    act_rot = jnp.dot(act_tokens, act_cols, preferred_element_type=jnp.float32).astype(jnp.bfloat16)
    grad_rot = jnp.dot(grad_tokens, grad_cols, preferred_element_type=jnp.float32).astype(jnp.bfloat16)
    query_weight = jnp.where(positions >= PROMPT, 1.0, 0.0).astype(jnp.bfloat16)
    grad_kept = grad_rot * query_weight[:, None]
    grad_all = lax.all_gather(grad_kept, "wb", axis=1, tiled=True)
    partial_rows = lax.dot_general(
        act_rot, grad_all, (((0,), (0,)), ((), ())), preferred_element_type=jnp.float32
    )
    gradient_rows = lax.psum_scatter(partial_rows, "wa", scatter_dimension=0, tiled=True)
    na, nb = lax.axis_size("wa"), lax.axis_size("wb")
    rows = gradient_rows.shape[0]
    gradient_rows = gradient_rows.reshape(rows, nb, na, -1).transpose(0, 2, 1, 3).reshape(rows, -1)
    query_gradient = lax.all_gather(gradient_rows.astype(jnp.bfloat16), WIDE, axis=0, tiled=True)
    eig_full = lax.all_gather(eig_values, WIDE, axis=0, tiled=True)
    eig_in, eig_out = eig_full.shape
    mean_eig = jnp.sum(eig_full.astype(jnp.float32)) / (eig_in * eig_out)
    dampings = mean_eig * jnp.exp2(damping_index.astype(jnp.float32) - 4.0)
    totals = score_rows(query_gradient, eig_full, dampings, train_act_rot, train_grad_rot)
    query_count = query_act.shape[0] * lax.axis_size(WIDE)
    factor = mean_eig * (1.0 / math.sqrt(float(query_count) * eig_in * eig_out))
    train_weight = jnp.where(train_positions >= PROMPT, 1.0, 0.0).astype(jnp.float32)
    return totals * factor * train_weight[None, :]


def split_wide(size):
    wb = 1
    while wb * wb < size and size % (wb * 2) == 0:
        wb *= 2
    return size // wb, wb


def solution(mesh):
    groups, wide = mesh.devices.shape
    wa, wb = split_wide(wide)
    grid = Mesh(mesh.devices.reshape(groups, wa, wb), ("groups",) + WIDE)
    tokens = ("groups",) + WIDE
    in_specs = (
        P(tokens, None),
        P(tokens, None),
        P(tokens),
        P(None, WIDE),
        P(None, WIDE),
        P(WIDE, None),
        P("groups"),
        P(None, WIDE),
        P(None, WIDE),
        P(WIDE),
    )
    out_specs = P("groups", WIDE)
    return jax.shard_map(shards, mesh=grid, in_specs=in_specs, out_specs=out_specs, check_vma=False)
```

```python
import math

import jax
import jax.numpy as jnp
from jax import lax
from jax.sharding import Mesh
from jax.sharding import PartitionSpec as P

PROMPT = 1024
WIDE = ("wa", "wb")


def score_rows(grad_rows, eig_rows, dampings, train_act_rot, train_grad_rot):
    acts_rows = train_act_rot.astype(jnp.float32)
    grad_wide = grad_rows.astype(jnp.float32)
    eig_wide = eig_rows.astype(jnp.float32)
    results = []
    for damping in range(dampings.shape[0]):
        precond = (grad_wide / (eig_wide + dampings[damping])).astype(jnp.bfloat16)
        projected = jnp.dot(precond, train_grad_rot, preferred_element_type=jnp.float32)
        results.append(jnp.sum(projected * acts_rows, axis=0))
    return jnp.stack(results)


def ring_gather(x, axis):
    n = lax.axis_size(axis)
    parts = [x]
    for shift in range(1, n):
        parts.append(lax.ppermute(x, axis, perm=[(i, (i + shift) % n) for i in range(n)]))
    return jnp.stack(parts)


def natural_order(stacked, axis):
    n = stacked.shape[0]
    reverse = stacked[::-1]
    doubled = jnp.concatenate([reverse, reverse], axis=0)
    return lax.dynamic_slice_in_dim(doubled, n - 1 - lax.axis_index(axis), n, axis=0)


def shards(
    query_act,
    query_grad,
    query_positions,
    act_basis,
    grad_basis,
    eig_values,
    damping_index,
    train_act_rot,
    train_grad_rot,
    train_positions,
):
    nb = lax.axis_size("wb")
    act_tokens = ring_gather(query_act, "wb")
    grad_tokens = ring_gather(query_grad, "wb")
    positions = ring_gather(query_positions, "wb")
    act_cols = lax.all_gather(act_basis, "wa", axis=1, tiled=True)
    grad_cols = lax.all_gather(grad_basis, "wa", axis=1, tiled=True)
    count = query_act.shape[0]
    act_rot = jnp.dot(
        act_tokens.reshape(nb * count, -1), act_cols, preferred_element_type=jnp.float32
    ).astype(jnp.bfloat16)
    grad_rot = jnp.dot(
        grad_tokens.reshape(nb * count, -1), grad_cols, preferred_element_type=jnp.float32
    ).astype(jnp.bfloat16)
    query_weight = jnp.where(positions.reshape(-1) >= PROMPT, 1.0, 0.0).astype(jnp.bfloat16)
    grad_kept = grad_rot * query_weight[:, None]
    act_rot = natural_order(act_rot.reshape(nb, count, -1), "wb").reshape(nb * count, -1)
    grad_kept = natural_order(grad_kept.reshape(nb, count, -1), "wb").reshape(nb * count, -1)
    grad_all = lax.all_gather(grad_kept, "wb", axis=1, tiled=True)
    partial_rows = lax.dot_general(
        act_rot, grad_all, (((0,), (0,)), ((), ())), preferred_element_type=jnp.float32
    )
    gradient_rows = lax.psum_scatter(partial_rows, "wa", scatter_dimension=0, tiled=True)
    na = lax.axis_size("wa")
    rows = gradient_rows.shape[0]
    gradient_rows = gradient_rows.reshape(rows, nb, na, -1).transpose(0, 2, 1, 3).reshape(rows, -1)
    query_gradient = lax.all_gather(gradient_rows.astype(jnp.bfloat16), WIDE, axis=0, tiled=True)
    eig_full = lax.all_gather(eig_values, WIDE, axis=0, tiled=True)
    eig_in, eig_out = eig_full.shape
    mean_eig = jnp.sum(eig_full.astype(jnp.float32)) / (eig_in * eig_out)
    dampings = mean_eig * jnp.exp2(damping_index.astype(jnp.float32) - 4.0)
    totals = score_rows(query_gradient, eig_full, dampings, train_act_rot, train_grad_rot)
    query_count = query_act.shape[0] * lax.axis_size(WIDE)
    factor = mean_eig * (1.0 / math.sqrt(float(query_count) * eig_in * eig_out))
    train_weight = jnp.where(train_positions >= PROMPT, 1.0, 0.0).astype(jnp.float32)
    return totals * factor * train_weight[None, :]


def split_wide(size):
    wb = 1
    while wb * wb < size and size % (wb * 2) == 0:
        wb *= 2
    return size // wb, wb


def solution(mesh):
    groups, wide = mesh.devices.shape
    wa, wb = split_wide(wide)
    grid = Mesh(mesh.devices.reshape(groups, wa, wb), ("groups",) + WIDE)
    tokens = ("groups",) + WIDE
    in_specs = (
        P(tokens, None),
        P(tokens, None),
        P(tokens),
        P(None, WIDE),
        P(None, WIDE),
        P(WIDE, None),
        P("groups"),
        P(None, WIDE),
        P(None, WIDE),
        P(WIDE),
    )
    out_specs = P("groups", WIDE)
    return jax.shard_map(shards, mesh=grid, in_specs=in_specs, out_specs=out_specs, check_vma=False)
```

```python
import math

import jax
import jax.numpy as jnp
from jax import lax
from jax.sharding import Mesh
from jax.sharding import PartitionSpec as P

PROMPT = 1024
WIDE = ("wa", "wy", "wc")
TOKENS = ("wy", "wc")
LINKS = ("wa", "wy")


def score_rows(grad_rows, eig_rows, dampings, train_act_rot, train_grad_rot):
    acts_rows = train_act_rot.astype(jnp.float32)
    grad_wide = grad_rows.astype(jnp.float32)
    eig_wide = eig_rows.astype(jnp.float32)
    results = []
    for damping in range(dampings.shape[0]):
        precond = (grad_wide / (eig_wide + dampings[damping])).astype(jnp.bfloat16)
        projected = jnp.dot(precond, train_grad_rot, preferred_element_type=jnp.float32)
        results.append(jnp.sum(projected * acts_rows, axis=0))
    return jnp.stack(results)


def ring_gather(x, axis):
    n = lax.axis_size(axis)
    parts = [x]
    for shift in range(1, n):
        parts.append(lax.ppermute(x, axis, perm=[(i, (i + shift) % n) for i in range(n)]))
    return jnp.stack(parts)


def natural_order(stacked, axis):
    n = stacked.shape[0]
    reverse = stacked[::-1]
    doubled = jnp.concatenate([reverse, reverse], axis=0)
    return lax.dynamic_slice_in_dim(doubled, n - 1 - lax.axis_index(axis), n, axis=0)


def shards(
    query_act,
    query_grad,
    query_positions,
    act_basis,
    grad_basis,
    eig_values,
    damping_index,
    train_act_rot,
    train_grad_rot,
    train_positions,
):
    nb = lax.axis_size(TOKENS)
    act_tokens = ring_gather(query_act, TOKENS)
    grad_tokens = ring_gather(query_grad, TOKENS)
    positions = ring_gather(query_positions, TOKENS)
    act_cols = lax.all_gather(act_basis, "wa", axis=1, tiled=True)
    grad_cols = lax.all_gather(grad_basis, "wa", axis=1, tiled=True)
    count = query_act.shape[0]
    act_rot = jnp.dot(
        act_tokens.reshape(nb * count, -1), act_cols, preferred_element_type=jnp.float32
    ).astype(jnp.bfloat16)
    grad_rot = jnp.dot(
        grad_tokens.reshape(nb * count, -1), grad_cols, preferred_element_type=jnp.float32
    ).astype(jnp.bfloat16)
    query_weight = jnp.where(positions.reshape(-1) >= PROMPT, 1.0, 0.0).astype(jnp.bfloat16)
    grad_kept = grad_rot * query_weight[:, None]
    act_rot = natural_order(act_rot.reshape(nb, count, -1), TOKENS).reshape(nb * count, -1)
    grad_kept = natural_order(grad_kept.reshape(nb, count, -1), TOKENS).reshape(nb * count, -1)
    grad_all = lax.all_gather(grad_kept, TOKENS, axis=1, tiled=True)
    partial_rows = lax.dot_general(
        act_rot, grad_all, (((0,), (0,)), ((), ())), preferred_element_type=jnp.float32
    )
    gradient_rows = lax.psum_scatter(partial_rows, "wa", scatter_dimension=0, tiled=True)
    na = lax.axis_size("wa")
    rows = gradient_rows.shape[0]
    gradient_rows = gradient_rows.reshape(rows, nb, na, -1).transpose(0, 2, 1, 3).reshape(rows, -1)
    query_gradient = lax.all_gather(
        lax.all_gather(gradient_rows.astype(jnp.bfloat16), LINKS, axis=0, tiled=True),
        "wc", axis=0, tiled=True,
    )
    eig_full = lax.all_gather(
        lax.all_gather(eig_values, LINKS, axis=0, tiled=True), "wc", axis=0, tiled=True
    )
    eig_in, eig_out = eig_full.shape
    mean_eig = jnp.sum(eig_full.astype(jnp.float32)) / (eig_in * eig_out)
    dampings = mean_eig * jnp.exp2(damping_index.astype(jnp.float32) - 4.0)
    cores = lax.axis_size("wc")
    block = eig_values.shape[0]
    acts_order = (
        train_act_rot.reshape(eig_in // (cores * block), cores, block, -1)
        .transpose(1, 0, 2, 3)
        .reshape(eig_in, -1)
    )
    totals = score_rows(query_gradient, eig_full, dampings, acts_order, train_grad_rot)
    query_count = query_act.shape[0] * lax.axis_size(WIDE)
    factor = mean_eig * (1.0 / math.sqrt(float(query_count) * eig_in * eig_out))
    train_weight = jnp.where(train_positions >= PROMPT, 1.0, 0.0).astype(jnp.float32)
    return totals * factor * train_weight[None, :]


def split_wide(size):
    wb = 1
    while wb * wb < size and size % (wb * 2) == 0:
        wb *= 2
    return size // wb, wb


def solution(mesh):
    groups, wide = mesh.devices.shape
    wa, wb = split_wide(wide)
    wc = 2 if wb % 2 == 0 else 1
    grid = Mesh(mesh.devices.reshape(groups, wa, wb // wc, wc), ("groups",) + WIDE)
    tokens = ("groups",) + WIDE
    in_specs = (
        P(tokens, None),
        P(tokens, None),
        P(tokens),
        P(None, WIDE),
        P(None, WIDE),
        P(WIDE, None),
        P("groups"),
        P(None, WIDE),
        P(None, WIDE),
        P(WIDE),
    )
    out_specs = P("groups", WIDE)
    return jax.shard_map(shards, mesh=grid, in_specs=in_specs, out_specs=out_specs, check_vma=False)
```

```python
import math

import jax
import jax.numpy as jnp
from jax import lax
from jax.sharding import Mesh
from jax.sharding import PartitionSpec as P

PROMPT = 1024
WIDE = ("wa", "wb")


def score_rows(grad_rows, eig_rows, dampings, train_act_rot, train_grad_rot):
    acts_rows = train_act_rot.astype(jnp.float32)
    grad_wide = grad_rows.astype(jnp.float32)
    eig_wide = eig_rows.astype(jnp.float32)
    results = []
    for damping in range(dampings.shape[0]):
        precond = (grad_wide / (eig_wide + dampings[damping])).astype(jnp.bfloat16)
        projected = jnp.dot(precond, train_grad_rot, preferred_element_type=jnp.float32)
        results.append(jnp.sum(projected * acts_rows, axis=0))
    return jnp.stack(results)


def ring_gather(x, axis):
    n = lax.axis_size(axis)
    parts = [x]
    for shift in range(1, n):
        parts.append(lax.ppermute(x, axis, perm=[(i, (i + shift) % n) for i in range(n)]))
    return jnp.stack(parts)


def natural_order(stacked, axis):
    n = stacked.shape[0]
    reverse = stacked[::-1]
    doubled = jnp.concatenate([reverse, reverse], axis=0)
    return lax.dynamic_slice_in_dim(doubled, n - 1 - lax.axis_index(axis), n, axis=0)


def shards(
    query_act,
    query_grad,
    query_positions,
    act_basis,
    grad_basis,
    eig_values,
    damping_index,
    train_act_rot,
    train_grad_rot,
    train_positions,
):
    nb = lax.axis_size("wb")
    act_tokens = ring_gather(query_act, "wb")
    grad_tokens = ring_gather(query_grad, "wb")
    positions = ring_gather(query_positions, "wb")
    act_cols = lax.all_gather(act_basis, "wa", axis=1, tiled=True)
    grad_cols = lax.all_gather(grad_basis, "wa", axis=1, tiled=True)
    count = query_act.shape[0]
    act_rot = jnp.dot(
        act_tokens.reshape(nb * count, -1), act_cols, preferred_element_type=jnp.float32
    ).astype(jnp.bfloat16)
    grad_rot = jnp.dot(
        grad_tokens.reshape(nb * count, -1), grad_cols, preferred_element_type=jnp.float32
    ).astype(jnp.bfloat16)
    query_weight = jnp.where(positions.reshape(-1) >= PROMPT, 1.0, 0.0).astype(jnp.bfloat16)
    grad_kept = grad_rot * query_weight[:, None]
    act_rot = natural_order(act_rot.reshape(nb, count, -1), "wb").reshape(nb * count, -1)
    grad_kept = natural_order(grad_kept.reshape(nb, count, -1), "wb").reshape(nb * count, -1)
    grad_all = lax.all_gather(grad_kept, "wb", axis=1, tiled=True)
    partial_rows = lax.dot_general(
        act_rot, grad_all, (((0,), (0,)), ((), ())), preferred_element_type=jnp.float32
    )
    gradient_rows = lax.psum_scatter(partial_rows, "wa", scatter_dimension=0, tiled=True)
    na = lax.axis_size("wa")
    rows = gradient_rows.shape[0]
    gradient_rows = gradient_rows.reshape(rows, nb, na, -1).transpose(0, 2, 1, 3).reshape(rows, -1)
    query_gradient = lax.all_gather(gradient_rows.astype(jnp.bfloat16), WIDE, axis=0, tiled=True)
    group_count = lax.axis_size("groups")
    eig_in, eig_out = eig_values.shape[0] * lax.axis_size(WIDE), eig_values.shape[1]
    width = eig_out // group_count
    my_cols = lax.dynamic_slice_in_dim(eig_values, lax.axis_index("groups") * width, width, axis=1)
    eig_part = lax.all_gather(my_cols, WIDE, axis=0, tiled=True)
    eig_parts = natural_order(ring_gather(eig_part, "groups"), "groups")
    eig_full = eig_parts.transpose(1, 0, 2).reshape(eig_in, eig_out)
    mean_eig = jnp.sum(eig_full.astype(jnp.float32)) / (eig_in * eig_out)
    dampings = mean_eig * jnp.exp2(damping_index.astype(jnp.float32) - 4.0)
    totals = score_rows(query_gradient, eig_full, dampings, train_act_rot, train_grad_rot)
    query_count = query_act.shape[0] * lax.axis_size(WIDE)
    factor = mean_eig * (1.0 / math.sqrt(float(query_count) * eig_in * eig_out))
    train_weight = jnp.where(train_positions >= PROMPT, 1.0, 0.0).astype(jnp.float32)
    return totals * factor * train_weight[None, :]


def split_wide(size):
    wb = 1
    while wb * wb < size and size % (wb * 2) == 0:
        wb *= 2
    return size // wb, wb


def solution(mesh):
    groups, wide = mesh.devices.shape
    wa, wb = split_wide(wide)
    grid = Mesh(mesh.devices.reshape(groups, wa, wb), ("groups",) + WIDE)
    tokens = ("groups",) + WIDE
    in_specs = (
        P(tokens, None),
        P(tokens, None),
        P(tokens),
        P(None, WIDE),
        P(None, WIDE),
        P(WIDE, None),
        P("groups"),
        P(None, WIDE),
        P(None, WIDE),
        P(WIDE),
    )
    out_specs = P("groups", WIDE)
    return jax.shard_map(shards, mesh=grid, in_specs=in_specs, out_specs=out_specs, check_vma=False)
```

```python
import math

import jax
import jax.numpy as jnp
from jax import lax
from jax.sharding import Mesh
from jax.sharding import PartitionSpec as P

PROMPT = 1024
WIDE = ("wa", "wb")


def score_rows(grad_rows, eig_rows, dampings, train_act_rot, train_grad_rot):
    acts_rows = train_act_rot.astype(jnp.float32)
    grad_wide = grad_rows.astype(jnp.float32)
    eig_wide = eig_rows.astype(jnp.float32)
    results = []
    for damping in range(dampings.shape[0]):
        precond = (grad_wide / (eig_wide + dampings[damping])).astype(jnp.bfloat16)
        projected = jnp.dot(precond, train_grad_rot, preferred_element_type=jnp.float32)
        results.append(jnp.sum(projected * acts_rows, axis=0))
    return jnp.stack(results)


def ring_gather(x, axis):
    n = lax.axis_size(axis)
    parts = [x]
    for shift in range(1, n):
        parts.append(lax.ppermute(x, axis, perm=[(i, (i + shift) % n) for i in range(n)]))
    return jnp.stack(parts)


def natural_order(stacked, axis):
    n = stacked.shape[0]
    reverse = stacked[::-1]
    doubled = jnp.concatenate([reverse, reverse], axis=0)
    return lax.dynamic_slice_in_dim(doubled, n - 1 - lax.axis_index(axis), n, axis=0)


def shards(
    query_act,
    query_grad,
    query_positions,
    act_basis,
    grad_basis,
    eig_values,
    damping_index,
    train_act_rot,
    train_grad_rot,
    train_positions,
):
    nb = lax.axis_size("wb")
    act_tokens = ring_gather(query_act, "wb")
    grad_tokens = ring_gather(query_grad, "wb")
    positions = ring_gather(query_positions, "wb")
    act_cols = lax.all_gather(act_basis, "wa", axis=1, tiled=True)
    grad_cols = lax.all_gather(grad_basis, "wa", axis=1, tiled=True)
    count = query_act.shape[0]
    act_rot = jnp.dot(
        act_tokens.reshape(nb * count, -1), act_cols, preferred_element_type=jnp.float32
    ).astype(jnp.bfloat16)
    grad_rot = jnp.dot(
        grad_tokens.reshape(nb * count, -1), grad_cols, preferred_element_type=jnp.float32
    ).astype(jnp.bfloat16)
    query_weight = jnp.where(positions.reshape(-1) >= PROMPT, 1.0, 0.0).astype(jnp.bfloat16)
    grad_kept = grad_rot * query_weight[:, None]
    act_rot = natural_order(act_rot.reshape(nb, count, -1), "wb").reshape(nb * count, -1)
    grad_kept = natural_order(grad_kept.reshape(nb, count, -1), "wb").reshape(nb * count, -1)
    grad_all = jnp.concatenate(list(ring_gather(grad_kept, "wb")), axis=1)
    partial_rows = lax.dot_general(
        act_rot, grad_all, (((0,), (0,)), ((), ())), preferred_element_type=jnp.float32
    )
    gradient_rows = lax.psum_scatter(partial_rows, "wa", scatter_dimension=0, tiled=True)
    na = lax.axis_size("wa")
    rows = gradient_rows.shape[0]
    by_shift = gradient_rows.reshape(rows, nb, na, -1).transpose(1, 0, 2, 3)
    gradient_rows = natural_order(by_shift, "wb").transpose(1, 2, 0, 3).reshape(rows, -1)
    query_gradient = ring_gather(gradient_rows.astype(jnp.bfloat16), WIDE)
    eig_full = ring_gather(eig_values, WIDE)
    blocks, block, eig_out = eig_full.shape
    eig_in = blocks * block
    query_gradient = query_gradient.reshape(eig_in, eig_out)
    eig_full = eig_full.reshape(eig_in, eig_out)
    acts_blocks = train_act_rot.reshape(blocks, block, -1)
    doubled = jnp.concatenate([acts_blocks, acts_blocks], axis=0)
    acts_order = lax.dynamic_slice_in_dim(doubled, lax.axis_index(WIDE) + 1, blocks, axis=0)[::-1]
    acts_order = acts_order.reshape(eig_in, -1)
    mean_eig = jnp.sum(eig_full.astype(jnp.float32)) / (eig_in * eig_out)
    dampings = mean_eig * jnp.exp2(damping_index.astype(jnp.float32) - 4.0)
    totals = score_rows(query_gradient, eig_full, dampings, acts_order, train_grad_rot)
    query_count = query_act.shape[0] * lax.axis_size(WIDE)
    factor = mean_eig * (1.0 / math.sqrt(float(query_count) * eig_in * eig_out))
    train_weight = jnp.where(train_positions >= PROMPT, 1.0, 0.0).astype(jnp.float32)
    return totals * factor * train_weight[None, :]


def split_wide(size):
    wb = 1
    while wb * wb < size and size % (wb * 2) == 0:
        wb *= 2
    return size // wb, wb


def solution(mesh):
    groups, wide = mesh.devices.shape
    wa, wb = split_wide(wide)
    grid = Mesh(mesh.devices.reshape(groups, wa, wb), ("groups",) + WIDE)
    tokens = ("groups",) + WIDE
    in_specs = (
        P(tokens, None),
        P(tokens, None),
        P(tokens),
        P(None, WIDE),
        P(None, WIDE),
        P(WIDE, None),
        P("groups"),
        P(None, WIDE),
        P(None, WIDE),
        P(WIDE),
    )
    out_specs = P("groups", WIDE)
    return jax.shard_map(shards, mesh=grid, in_specs=in_specs, out_specs=out_specs, check_vma=False)
```

```python
import math

import jax
import jax.numpy as jnp
from jax import lax
from jax.sharding import Mesh
from jax.sharding import PartitionSpec as P

PROMPT = 1024
WIDE = ("wa", "wb")


def score_rows(grad_rows, eig_rows, dampings, train_act_rot, train_grad_rot):
    acts_rows = train_act_rot.astype(jnp.float32)
    grad_wide = grad_rows.astype(jnp.float32)
    eig_wide = eig_rows.astype(jnp.float32)
    results = []
    for damping in range(dampings.shape[0]):
        precond = (grad_wide / (eig_wide + dampings[damping])).astype(jnp.bfloat16)
        projected = jnp.dot(precond, train_grad_rot, preferred_element_type=jnp.float32)
        results.append(jnp.sum(projected * acts_rows, axis=0))
    return jnp.stack(results)


def ring_gather(x, axis):
    n = lax.axis_size(axis)
    parts = [x]
    for shift in range(1, n):
        parts.append(lax.ppermute(x, axis, perm=[(i, (i + shift) % n) for i in range(n)]))
    return jnp.stack(parts)


def natural_order(stacked, axis):
    n = stacked.shape[0]
    reverse = stacked[::-1]
    doubled = jnp.concatenate([reverse, reverse], axis=0)
    return lax.dynamic_slice_in_dim(doubled, n - 1 - lax.axis_index(axis), n, axis=0)


def shards(
    query_act,
    query_grad,
    query_positions,
    act_basis,
    grad_basis,
    eig_values,
    damping_index,
    train_act_rot,
    train_grad_rot,
    train_positions,
):
    nb = lax.axis_size("wb")
    act_tokens = ring_gather(query_act, "wb")
    grad_tokens = ring_gather(query_grad, "wb")
    positions = ring_gather(query_positions, "wb")
    act_cols = lax.all_gather(act_basis, "wa", axis=1, tiled=True)
    grad_cols = lax.all_gather(grad_basis, "wa", axis=1, tiled=True)
    count = query_act.shape[0]
    act_rot = jnp.dot(
        act_tokens.reshape(nb * count, -1), act_cols, preferred_element_type=jnp.float32
    ).astype(jnp.bfloat16)
    grad_rot = jnp.dot(
        grad_tokens.reshape(nb * count, -1), grad_cols, preferred_element_type=jnp.float32
    ).astype(jnp.bfloat16)
    query_weight = jnp.where(positions.reshape(-1) >= PROMPT, 1.0, 0.0).astype(jnp.bfloat16)
    grad_kept = grad_rot * query_weight[:, None]
    act_rot = natural_order(act_rot.reshape(nb, count, -1), "wb").reshape(nb * count, -1)
    grad_kept = natural_order(grad_kept.reshape(nb, count, -1), "wb").reshape(nb * count, -1)
    grad_all = lax.all_gather(grad_kept, "wb", axis=1, tiled=True)
    partial_rows = lax.dot_general(
        act_rot, grad_all, (((0,), (0,)), ((), ())), preferred_element_type=jnp.float32
    )
    gradient_rows = lax.psum_scatter(partial_rows, "wa", scatter_dimension=0, tiled=True)
    na = lax.axis_size("wa")
    rows = gradient_rows.shape[0]
    gradient_rows = gradient_rows.reshape(rows, nb, na, -1).transpose(0, 2, 1, 3).reshape(rows, -1)
    eig_in = eig_values.shape[0] * lax.axis_size(WIDE)
    eig_out = eig_values.shape[1]
    eig_total = lax.psum(jnp.sum(eig_values.astype(jnp.float32)), WIDE)
    mean_eig = eig_total / (eig_in * eig_out)
    dampings = mean_eig * jnp.exp2(damping_index.astype(jnp.float32) - 4.0)
    payload = jnp.concatenate([gradient_rows.astype(jnp.bfloat16), eig_values], axis=1)
    rows_held = lax.all_gather(payload, "wa", axis=0, tiled=True)
    gradient_held, eig_held = rows_held[:, :eig_out], rows_held[:, eig_out:]
    grads_near = ring_gather(train_grad_rot, "wb")
    me = lax.axis_index("wb")
    act_blocks = train_act_rot.reshape(na, nb, -1, train_act_rot.shape[1])
    acts_near = [act_blocks[:, me]]
    for shift in range(1, nb):
        outgoing = lax.dynamic_index_in_dim(act_blocks, (me + shift) % nb, axis=1, keepdims=False)
        acts_near.append(lax.ppermute(outgoing, "wb", perm=[(i, (i + shift) % nb) for i in range(nb)]))
    acts_near = jnp.stack(acts_near).reshape(nb, na * act_blocks.shape[2], -1).astype(jnp.float32)
    grad_wide = gradient_held.astype(jnp.float32)
    eig_wide = eig_held.astype(jnp.float32)
    results = []
    for damping in range(dampings.shape[0]):
        precond = (grad_wide / (eig_wide + dampings[damping])).astype(jnp.bfloat16)
        projected = jnp.einsum("ij,sjt->sit", precond, grads_near, preferred_element_type=jnp.float32)
        results.append(jnp.sum(projected * acts_near, axis=1))
    partial = jnp.stack(results, axis=1)
    totals = partial[0]
    for shift in range(1, nb):
        totals = totals + lax.ppermute(partial[shift], "wb", perm=[(i, (i - shift) % nb) for i in range(nb)])
    query_count = query_act.shape[0] * lax.axis_size(WIDE)
    factor = mean_eig * (1.0 / math.sqrt(float(query_count) * eig_in * eig_out))
    train_weight = jnp.where(train_positions >= PROMPT, 1.0, 0.0).astype(jnp.float32)
    return totals * factor * train_weight[None, :]

def split_wide(size):
    wb = 1
    while wb * wb < size and size % (wb * 2) == 0:
        wb *= 2
    return size // wb, wb


def solution(mesh):
    groups, wide = mesh.devices.shape
    wa, wb = split_wide(wide)
    grid = Mesh(mesh.devices.reshape(groups, wa, wb), ("groups",) + WIDE)
    tokens = ("groups",) + WIDE
    in_specs = (
        P(tokens, None),
        P(tokens, None),
        P(tokens),
        P(None, WIDE),
        P(None, WIDE),
        P(WIDE, None),
        P("groups"),
        P(None, WIDE),
        P(None, WIDE),
        P(WIDE),
    )
    out_specs = P("groups", WIDE)
    return jax.shard_map(shards, mesh=grid, in_specs=in_specs, out_specs=out_specs, check_vma=False)
```

```python
import math

import jax
import jax.numpy as jnp
from jax import lax
from jax.sharding import Mesh
from jax.sharding import PartitionSpec as P

PROMPT = 1024
WIDE = ("wa", "wb")


def score_rows(grad_rows, eig_rows, dampings, train_act_rot, train_grad_rot):
    acts_rows = train_act_rot.astype(jnp.float32)
    grad_wide = grad_rows.astype(jnp.float32)
    eig_wide = eig_rows.astype(jnp.float32)
    results = []
    for damping in range(dampings.shape[0]):
        precond = (grad_wide / (eig_wide + dampings[damping])).astype(jnp.bfloat16)
        projected = jnp.dot(precond, train_grad_rot, preferred_element_type=jnp.float32)
        results.append(jnp.sum(projected * acts_rows, axis=0))
    return jnp.stack(results)


def ring_gather(x, axis):
    n = lax.axis_size(axis)
    parts = [x]
    for shift in range(1, n):
        parts.append(lax.ppermute(x, axis, perm=[(i, (i + shift) % n) for i in range(n)]))
    return jnp.stack(parts)


def natural_order(stacked, axis):
    n = stacked.shape[0]
    reverse = stacked[::-1]
    doubled = jnp.concatenate([reverse, reverse], axis=0)
    return lax.dynamic_slice_in_dim(doubled, n - 1 - lax.axis_index(axis), n, axis=0)


def shards(
    query_act,
    query_grad,
    query_positions,
    act_basis,
    grad_basis,
    eig_values,
    damping_index,
    train_act_rot,
    train_grad_rot,
    train_positions,
):
    nb = lax.axis_size("wb")
    na = lax.axis_size("wa")
    act_tokens = ring_gather(query_act, "wb")
    grad_tokens = ring_gather(query_grad, "wb")
    positions = ring_gather(query_positions, "wb")
    eig_total = lax.psum(jnp.sum(eig_values.astype(jnp.float32)), WIDE)
    eig_total, grad_tokens = lax.optimization_barrier((eig_total, grad_tokens))
    me = lax.axis_index("wb")
    half = train_grad_rot.shape[0] // 2
    first_rows, train_act_rot, _ = lax.optimization_barrier((train_grad_rot[:half], train_act_rot, grad_tokens))
    grads_first = ring_gather(first_rows, "wb")
    act_blocks = train_act_rot.reshape(na, nb, -1, train_act_rot.shape[1])
    acts_near = [act_blocks[:, me]]
    for shift in range(1, nb):
        outgoing = lax.dynamic_index_in_dim(act_blocks, (me + shift) % nb, axis=1, keepdims=False)
        acts_near.append(lax.ppermute(outgoing, "wb", perm=[(i, (i + shift) % nb) for i in range(nb)]))
    acts_near = jnp.stack(acts_near)
    act_cols = lax.all_gather(act_basis, "wa", axis=1, tiled=True)
    grad_cols = lax.all_gather(grad_basis, "wa", axis=1, tiled=True)
    count = query_act.shape[0]
    act_rot = jnp.dot(
        act_tokens.reshape(nb * count, -1), act_cols, preferred_element_type=jnp.float32
    ).astype(jnp.bfloat16)
    grad_rot = jnp.dot(
        grad_tokens.reshape(nb * count, -1), grad_cols, preferred_element_type=jnp.float32
    ).astype(jnp.bfloat16)
    query_weight = jnp.where(positions.reshape(-1) >= PROMPT, 1.0, 0.0).astype(jnp.bfloat16)
    grad_kept = grad_rot * query_weight[:, None]
    act_rot = natural_order(act_rot.reshape(nb, count, -1), "wb").reshape(nb * count, -1)
    grad_kept = natural_order(grad_kept.reshape(nb, count, -1), "wb").reshape(nb * count, -1)
    grads_first, acts_near, grad_kept = lax.optimization_barrier((grads_first, acts_near, grad_kept))
    second_rows, _ = lax.optimization_barrier((train_grad_rot[half:], grad_kept))
    grads_second = ring_gather(second_rows, "wb")
    grad_all = lax.all_gather(grad_kept, "wb", axis=1, tiled=True)
    partial_rows = lax.dot_general(
        act_rot, grad_all, (((0,), (0,)), ((), ())), preferred_element_type=jnp.float32
    )
    gradient_rows = lax.psum_scatter(partial_rows, "wa", scatter_dimension=0, tiled=True)
    rows = gradient_rows.shape[0]
    gradient_rows = gradient_rows.reshape(rows, nb, na, -1).transpose(0, 2, 1, 3).reshape(rows, -1)
    eig_in = eig_values.shape[0] * lax.axis_size(WIDE)
    eig_out = eig_values.shape[1]
    mean_eig = eig_total / (eig_in * eig_out)
    dampings = mean_eig * jnp.exp2(damping_index.astype(jnp.float32) - 4.0)
    payload = jnp.concatenate([gradient_rows.astype(jnp.bfloat16), eig_values], axis=1)
    grads_second, payload = lax.optimization_barrier((grads_second, payload))
    rows_held = lax.all_gather(payload, "wa", axis=0, tiled=True)
    gradient_held, eig_held = rows_held[:, :eig_out], rows_held[:, eig_out:]
    grads_near = jnp.concatenate([grads_first, grads_second], axis=1)
    acts_near = acts_near.reshape(nb, na * act_blocks.shape[2], -1).astype(jnp.float32)
    grad_wide = gradient_held.astype(jnp.float32)
    eig_wide = eig_held.astype(jnp.float32)
    results = []
    for damping in range(dampings.shape[0]):
        precond = (grad_wide / (eig_wide + dampings[damping])).astype(jnp.bfloat16)
        projected = jnp.einsum("ij,sjt->sit", precond, grads_near, preferred_element_type=jnp.float32)
        results.append(jnp.sum(projected * acts_near, axis=1))
    partial = jnp.stack(results, axis=1)
    totals = partial[0]
    for shift in range(1, nb):
        totals = totals + lax.ppermute(partial[shift], "wb", perm=[(i, (i - shift) % nb) for i in range(nb)])
    query_count = query_act.shape[0] * lax.axis_size(WIDE)
    factor = mean_eig * (1.0 / math.sqrt(float(query_count) * eig_in * eig_out))
    train_weight = jnp.where(train_positions >= PROMPT, 1.0, 0.0).astype(jnp.float32)
    return totals * factor * train_weight[None, :]

def split_wide(size):
    wb = 1
    while wb * wb < size and size % (wb * 2) == 0:
        wb *= 2
    return size // wb, wb


def solution(mesh):
    groups, wide = mesh.devices.shape
    wa, wb = split_wide(wide)
    grid = Mesh(mesh.devices.reshape(groups, wa, wb), ("groups",) + WIDE)
    tokens = ("groups",) + WIDE
    in_specs = (
        P(tokens, None),
        P(tokens, None),
        P(tokens),
        P(None, WIDE),
        P(None, WIDE),
        P(WIDE, None),
        P("groups"),
        P(None, WIDE),
        P(None, WIDE),
        P(WIDE),
    )
    out_specs = P("groups", WIDE)
    return jax.shard_map(shards, mesh=grid, in_specs=in_specs, out_specs=out_specs, check_vma=False)
```

```python
import math

import jax
import jax.numpy as jnp
from jax import lax
from jax.sharding import Mesh
from jax.sharding import PartitionSpec as P

PROMPT = 1024
WIDE = ("wa", "wb")


def score_rows(grad_rows, eig_rows, dampings, train_act_rot, train_grad_rot):
    acts_rows = train_act_rot.astype(jnp.float32)
    grad_wide = grad_rows.astype(jnp.float32)
    eig_wide = eig_rows.astype(jnp.float32)
    results = []
    for damping in range(dampings.shape[0]):
        precond = (grad_wide / (eig_wide + dampings[damping])).astype(jnp.bfloat16)
        projected = jnp.dot(precond, train_grad_rot, preferred_element_type=jnp.float32)
        results.append(jnp.sum(projected * acts_rows, axis=0))
    return jnp.stack(results)


def ring_gather(x, axis):
    n = lax.axis_size(axis)
    parts = [x]
    for shift in range(1, n):
        parts.append(lax.ppermute(x, axis, perm=[(i, (i + shift) % n) for i in range(n)]))
    return jnp.stack(parts)


def natural_order(stacked, axis):
    n = stacked.shape[0]
    reverse = stacked[::-1]
    doubled = jnp.concatenate([reverse, reverse], axis=0)
    return lax.dynamic_slice_in_dim(doubled, n - 1 - lax.axis_index(axis), n, axis=0)


def shards(
    query_act,
    query_grad,
    query_positions,
    act_basis,
    grad_basis,
    eig_values,
    damping_index,
    train_act_rot,
    train_grad_rot,
    train_positions,
):
    nb = lax.axis_size("wb")
    na = lax.axis_size("wa")
    act_tokens = ring_gather(query_act, "wb")
    grad_tokens = ring_gather(query_grad, "wb")
    positions = ring_gather(query_positions, "wb")
    me = lax.axis_index("wb")
    half = train_grad_rot.shape[0] // 2
    first_rows, train_act_rot, _ = lax.optimization_barrier((train_grad_rot[:half], train_act_rot, grad_tokens))
    grads_first = ring_gather(first_rows, "wb")
    act_blocks = train_act_rot.reshape(na, nb, -1, train_act_rot.shape[1])
    acts_near = [act_blocks[:, me]]
    for shift in range(1, nb):
        outgoing = lax.dynamic_index_in_dim(act_blocks, (me + shift) % nb, axis=1, keepdims=False)
        acts_near.append(lax.ppermute(outgoing, "wb", perm=[(i, (i + shift) % nb) for i in range(nb)]))
    acts_near = jnp.stack(acts_near)
    act_cols = lax.all_gather(act_basis, "wa", axis=1, tiled=True)
    grad_cols = lax.all_gather(grad_basis, "wa", axis=1, tiled=True)
    count = query_act.shape[0]
    act_rot = jnp.dot(
        act_tokens.reshape(nb * count, -1), act_cols, preferred_element_type=jnp.float32
    ).astype(jnp.bfloat16)
    grad_rot = jnp.dot(
        grad_tokens.reshape(nb * count, -1), grad_cols, preferred_element_type=jnp.float32
    ).astype(jnp.bfloat16)
    query_weight = jnp.where(positions.reshape(-1) >= PROMPT, 1.0, 0.0).astype(jnp.bfloat16)
    grad_kept = grad_rot * query_weight[:, None]
    act_rot = natural_order(act_rot.reshape(nb, count, -1), "wb").reshape(nb * count, -1)
    grad_kept = natural_order(grad_kept.reshape(nb, count, -1), "wb").reshape(nb * count, -1)
    grads_first, acts_near, grad_kept = lax.optimization_barrier((grads_first, acts_near, grad_kept))
    second_rows, _ = lax.optimization_barrier((train_grad_rot[half:], grad_kept))
    grads_second = ring_gather(second_rows, "wb")
    grad_all = lax.all_gather(grad_kept, "wb", axis=1, tiled=True)
    partial_rows = lax.dot_general(
        act_rot, grad_all, (((0,), (0,)), ((), ())), preferred_element_type=jnp.float32
    )
    eig_sum = jnp.sum(eig_values.astype(jnp.float32))
    group_sum = eig_sum
    for shift in range(1, nb):
        group_sum = group_sum + lax.ppermute(eig_sum, "wb", perm=[(i, (i + shift) % nb) for i in range(nb)])
    extra = jnp.broadcast_to(group_sum, (partial_rows.shape[0], 128))
    reduced = lax.psum_scatter(
        jnp.concatenate([partial_rows, extra], axis=1), "wa", scatter_dimension=0, tiled=True
    )
    gradient_rows = reduced[:, : partial_rows.shape[1]]
    eig_total = reduced[0, partial_rows.shape[1]]
    rows = gradient_rows.shape[0]
    gradient_rows = gradient_rows.reshape(rows, nb, na, -1).transpose(0, 2, 1, 3).reshape(rows, -1)
    eig_in = eig_values.shape[0] * lax.axis_size(WIDE)
    eig_out = eig_values.shape[1]
    mean_eig = eig_total / (eig_in * eig_out)
    dampings = mean_eig * jnp.exp2(damping_index.astype(jnp.float32) - 4.0)
    payload = jnp.concatenate([gradient_rows.astype(jnp.bfloat16), eig_values], axis=1)
    grads_second, payload = lax.optimization_barrier((grads_second, payload))
    rows_held = lax.all_gather(payload, "wa", axis=0, tiled=True)
    gradient_held, eig_held = rows_held[:, :eig_out], rows_held[:, eig_out:]
    grads_near = jnp.concatenate([grads_first, grads_second], axis=1)
    acts_near = acts_near.reshape(nb, na * act_blocks.shape[2], -1).astype(jnp.float32)
    grad_wide = gradient_held.astype(jnp.float32)
    eig_wide = eig_held.astype(jnp.float32)
    results = []
    for damping in range(dampings.shape[0]):
        precond = (grad_wide / (eig_wide + dampings[damping])).astype(jnp.bfloat16)
        projected = jnp.einsum("ij,sjt->sit", precond, grads_near, preferred_element_type=jnp.float32)
        results.append(jnp.sum(projected * acts_near, axis=1))
    partial = jnp.stack(results, axis=1)
    totals = partial[0]
    for shift in range(1, nb):
        totals = totals + lax.ppermute(partial[shift], "wb", perm=[(i, (i - shift) % nb) for i in range(nb)])
    query_count = query_act.shape[0] * lax.axis_size(WIDE)
    factor = mean_eig * (1.0 / math.sqrt(float(query_count) * eig_in * eig_out))
    train_weight = jnp.where(train_positions >= PROMPT, 1.0, 0.0).astype(jnp.float32)
    return totals * factor * train_weight[None, :]

def split_wide(size):
    wb = 1
    while wb * wb < size and size % (wb * 2) == 0:
        wb *= 2
    return size // wb, wb


def solution(mesh):
    groups, wide = mesh.devices.shape
    wa, wb = split_wide(wide)
    grid = Mesh(mesh.devices.reshape(groups, wa, wb), ("groups",) + WIDE)
    tokens = ("groups",) + WIDE
    in_specs = (
        P(tokens, None),
        P(tokens, None),
        P(tokens),
        P(None, WIDE),
        P(None, WIDE),
        P(WIDE, None),
        P("groups"),
        P(None, WIDE),
        P(None, WIDE),
        P(WIDE),
    )
    out_specs = P("groups", WIDE)
    return jax.shard_map(shards, mesh=grid, in_specs=in_specs, out_specs=out_specs, check_vma=False)
```

```python
import math

import jax
import jax.numpy as jnp
from jax import lax
from jax.sharding import Mesh
from jax.sharding import PartitionSpec as P

PROMPT = 1024
WIDE = ("wa", "wb")


def score_rows(grad_rows, eig_rows, dampings, train_act_rot, train_grad_rot):
    acts_rows = train_act_rot.astype(jnp.float32)
    grad_wide = grad_rows.astype(jnp.float32)
    eig_wide = eig_rows.astype(jnp.float32)
    results = []
    for damping in range(dampings.shape[0]):
        precond = (grad_wide / (eig_wide + dampings[damping])).astype(jnp.bfloat16)
        projected = jnp.dot(precond, train_grad_rot, preferred_element_type=jnp.float32)
        results.append(jnp.sum(projected * acts_rows, axis=0))
    return jnp.stack(results)


def ring_gather(x, axis):
    n = lax.axis_size(axis)
    parts = [x]
    for shift in range(1, n):
        parts.append(lax.ppermute(x, axis, perm=[(i, (i + shift) % n) for i in range(n)]))
    return jnp.stack(parts)


def natural_order(stacked, axis):
    n = stacked.shape[0]
    reverse = stacked[::-1]
    doubled = jnp.concatenate([reverse, reverse], axis=0)
    return lax.dynamic_slice_in_dim(doubled, n - 1 - lax.axis_index(axis), n, axis=0)


def shards(
    query_act,
    query_grad,
    query_positions,
    act_basis,
    grad_basis,
    eig_values,
    damping_index,
    train_act_rot,
    train_grad_rot,
    train_positions,
):
    nb = lax.axis_size("wb")
    na = lax.axis_size("wa")
    act_tokens = ring_gather(query_act, "wb")
    grad_tokens = ring_gather(query_grad, "wb")
    positions = ring_gather(query_positions, "wb")
    act_cols = lax.all_gather(act_basis, "wa", axis=1, tiled=True)
    grad_cols = lax.all_gather(grad_basis, "wa", axis=1, tiled=True)
    count = query_act.shape[0]
    act_rot = jnp.dot(
        act_tokens.reshape(nb * count, -1), act_cols, preferred_element_type=jnp.float32
    ).astype(jnp.bfloat16)
    grad_rot = jnp.dot(
        grad_tokens.reshape(nb * count, -1), grad_cols, preferred_element_type=jnp.float32
    ).astype(jnp.bfloat16)
    query_weight = jnp.where(positions.reshape(-1) >= PROMPT, 1.0, 0.0).astype(jnp.bfloat16)
    grad_kept = grad_rot * query_weight[:, None]
    act_rot = natural_order(act_rot.reshape(nb, count, -1), "wb").reshape(nb * count, -1)
    grad_kept = natural_order(grad_kept.reshape(nb, count, -1), "wb").reshape(nb * count, -1)
    grad_all = lax.all_gather(grad_kept, "wb", axis=1, tiled=True)
    partial_rows = lax.dot_general(
        act_rot, grad_all, (((0,), (0,)), ((), ())), preferred_element_type=jnp.float32
    )
    eig_sum = jnp.sum(eig_values.astype(jnp.float32))
    group_sum = eig_sum
    for shift in range(1, nb):
        group_sum = group_sum + lax.ppermute(eig_sum, "wb", perm=[(i, (i + shift) % nb) for i in range(nb)])
    extra = jnp.broadcast_to(group_sum, (partial_rows.shape[0], 128))
    reduced = lax.psum_scatter(
        jnp.concatenate([partial_rows, extra], axis=1), "wa", scatter_dimension=0, tiled=True
    )
    gradient_rows = reduced[:, : partial_rows.shape[1]]
    me = lax.axis_index("wb")
    half = train_grad_rot.shape[0] // 2
    first_rows, train_act_rot, _ = lax.optimization_barrier((train_grad_rot[:half], train_act_rot, partial_rows))
    grads_first = ring_gather(first_rows, "wb")
    act_blocks = train_act_rot.reshape(na, nb, -1, train_act_rot.shape[1])
    acts_near = [act_blocks[:, me]]
    for shift in range(1, nb):
        outgoing = lax.dynamic_index_in_dim(act_blocks, (me + shift) % nb, axis=1, keepdims=False)
        acts_near.append(lax.ppermute(outgoing, "wb", perm=[(i, (i + shift) % nb) for i in range(nb)]))
    acts_near = jnp.stack(acts_near)
    eig_total = reduced[0, partial_rows.shape[1]]
    rows = gradient_rows.shape[0]
    gradient_rows = gradient_rows.reshape(rows, nb, na, -1).transpose(0, 2, 1, 3).reshape(rows, -1)
    eig_in = eig_values.shape[0] * lax.axis_size(WIDE)
    eig_out = eig_values.shape[1]
    mean_eig = eig_total / (eig_in * eig_out)
    dampings = mean_eig * jnp.exp2(damping_index.astype(jnp.float32) - 4.0)
    payload = jnp.concatenate([gradient_rows.astype(jnp.bfloat16), eig_values], axis=1)
    grads_first, acts_near, payload = lax.optimization_barrier((grads_first, acts_near, payload))
    second_rows, _ = lax.optimization_barrier((train_grad_rot[half:], payload))
    grads_second = ring_gather(second_rows, "wb")
    rows_held = lax.all_gather(payload, "wa", axis=0, tiled=True)
    gradient_held, eig_held = rows_held[:, :eig_out], rows_held[:, eig_out:]
    grads_near = jnp.concatenate([grads_first, grads_second], axis=1)
    acts_near = acts_near.reshape(nb, na * act_blocks.shape[2], -1).astype(jnp.float32)
    grad_wide = gradient_held.astype(jnp.float32)
    eig_wide = eig_held.astype(jnp.float32)
    results = []
    for damping in range(dampings.shape[0]):
        precond = (grad_wide / (eig_wide + dampings[damping])).astype(jnp.bfloat16)
        projected = jnp.einsum("ij,sjt->sit", precond, grads_near, preferred_element_type=jnp.float32)
        results.append(jnp.sum(projected * acts_near, axis=1))
    partial = jnp.stack(results, axis=1)
    totals = partial[0]
    for shift in range(1, nb):
        totals = totals + lax.ppermute(partial[shift], "wb", perm=[(i, (i - shift) % nb) for i in range(nb)])
    query_count = query_act.shape[0] * lax.axis_size(WIDE)
    factor = mean_eig * (1.0 / math.sqrt(float(query_count) * eig_in * eig_out))
    train_weight = jnp.where(train_positions >= PROMPT, 1.0, 0.0).astype(jnp.float32)
    return totals * factor * train_weight[None, :]

def split_wide(size):
    wb = 1
    while wb * wb < size and size % (wb * 2) == 0:
        wb *= 2
    return size // wb, wb


def solution(mesh):
    groups, wide = mesh.devices.shape
    wa, wb = split_wide(wide)
    grid = Mesh(mesh.devices.reshape(groups, wa, wb), ("groups",) + WIDE)
    tokens = ("groups",) + WIDE
    in_specs = (
        P(tokens, None),
        P(tokens, None),
        P(tokens),
        P(None, WIDE),
        P(None, WIDE),
        P(WIDE, None),
        P("groups"),
        P(None, WIDE),
        P(None, WIDE),
        P(WIDE),
    )
    out_specs = P("groups", WIDE)
    return jax.shard_map(shards, mesh=grid, in_specs=in_specs, out_specs=out_specs, check_vma=False)
```

```python
import math

import jax
import jax.numpy as jnp
from jax import lax
from jax.sharding import Mesh
from jax.sharding import PartitionSpec as P

PROMPT = 1024
WIDE = ("wa", "wb")


def score_rows(grad_rows, eig_rows, dampings, train_act_rot, train_grad_rot):
    acts_rows = train_act_rot.astype(jnp.float32)
    grad_wide = grad_rows.astype(jnp.float32)
    eig_wide = eig_rows.astype(jnp.float32)
    results = []
    for damping in range(dampings.shape[0]):
        precond = (grad_wide / (eig_wide + dampings[damping])).astype(jnp.bfloat16)
        projected = jnp.dot(precond, train_grad_rot, preferred_element_type=jnp.float32)
        results.append(jnp.sum(projected * acts_rows, axis=0))
    return jnp.stack(results)


def ring_gather(x, axis):
    n = lax.axis_size(axis)
    parts = [x]
    for shift in range(1, n):
        parts.append(lax.ppermute(x, axis, perm=[(i, (i + shift) % n) for i in range(n)]))
    return jnp.stack(parts)


def natural_order(stacked, axis):
    n = stacked.shape[0]
    reverse = stacked[::-1]
    doubled = jnp.concatenate([reverse, reverse], axis=0)
    return lax.dynamic_slice_in_dim(doubled, n - 1 - lax.axis_index(axis), n, axis=0)


def shards(
    query_act,
    query_grad,
    query_positions,
    act_basis,
    grad_basis,
    eig_values,
    damping_index,
    train_act_rot,
    train_grad_rot,
    train_positions,
):
    nb = lax.axis_size("wb")
    na = lax.axis_size("wa")
    act_tokens = ring_gather(query_act, "wb")
    grad_tokens = ring_gather(query_grad, "wb")
    positions = ring_gather(query_positions, "wb")
    act_tokens, grad_tokens, positions = lax.optimization_barrier((act_tokens, grad_tokens, positions))
    act_cols = lax.all_gather(act_basis, "wa", axis=1, tiled=True)
    grad_cols = lax.all_gather(grad_basis, "wa", axis=1, tiled=True)
    count = query_act.shape[0]
    act_rot = jnp.dot(
        act_tokens.reshape(nb * count, -1), act_cols, preferred_element_type=jnp.float32
    ).astype(jnp.bfloat16)
    grad_rot = jnp.dot(
        grad_tokens.reshape(nb * count, -1), grad_cols, preferred_element_type=jnp.float32
    ).astype(jnp.bfloat16)
    query_weight = jnp.where(positions.reshape(-1) >= PROMPT, 1.0, 0.0).astype(jnp.bfloat16)
    grad_kept = grad_rot * query_weight[:, None]
    act_rot = natural_order(act_rot.reshape(nb, count, -1), "wb").reshape(nb * count, -1)
    grad_kept = natural_order(grad_kept.reshape(nb, count, -1), "wb").reshape(nb * count, -1)
    grad_all = jnp.concatenate(list(ring_gather(grad_kept, "wb")), axis=1)
    partial_rows = lax.dot_general(
        act_rot, grad_all, (((0,), (0,)), ((), ())), preferred_element_type=jnp.float32
    )
    eig_sum = jnp.sum(eig_values.astype(jnp.float32))
    group_sum = eig_sum
    for shift in range(1, nb):
        group_sum = group_sum + lax.ppermute(eig_sum, "wb", perm=[(i, (i + shift) % nb) for i in range(nb)])
    extra = jnp.broadcast_to(group_sum, (partial_rows.shape[0], 128))
    reduced = lax.psum_scatter(
        jnp.concatenate([partial_rows, extra], axis=1), "wa", scatter_dimension=0, tiled=True
    )
    rows = reduced.shape[0]
    by_shift = reduced[:, : partial_rows.shape[1]].reshape(rows, nb, na, -1).transpose(1, 0, 2, 3)
    gradient_rows = natural_order(by_shift, "wb").transpose(1, 2, 0, 3).reshape(rows, -1)
    me = lax.axis_index("wb")
    half = train_grad_rot.shape[0] // 2
    first_rows, train_act_rot, _ = lax.optimization_barrier((train_grad_rot[:half], train_act_rot, partial_rows))
    grads_first = ring_gather(first_rows, "wb")
    act_blocks = train_act_rot.reshape(na, nb, -1, train_act_rot.shape[1])
    acts_near = [act_blocks[:, me]]
    for shift in range(1, nb):
        outgoing = lax.dynamic_index_in_dim(act_blocks, (me + shift) % nb, axis=1, keepdims=False)
        acts_near.append(lax.ppermute(outgoing, "wb", perm=[(i, (i + shift) % nb) for i in range(nb)]))
    acts_near = jnp.stack(acts_near)
    eig_total = reduced[0, partial_rows.shape[1]]
    eig_in = eig_values.shape[0] * lax.axis_size(WIDE)
    eig_out = eig_values.shape[1]
    mean_eig = eig_total / (eig_in * eig_out)
    dampings = mean_eig * jnp.exp2(damping_index.astype(jnp.float32) - 4.0)
    payload = jnp.concatenate([gradient_rows.astype(jnp.bfloat16), eig_values], axis=1)
    grads_first, acts_near, payload = lax.optimization_barrier((grads_first, acts_near, payload))
    second_rows, _ = lax.optimization_barrier((train_grad_rot[half:], payload))
    grads_second = ring_gather(second_rows, "wb")
    rows_held = lax.all_gather(payload, "wa", axis=0, tiled=True)
    gradient_held, eig_held = rows_held[:, :eig_out], rows_held[:, eig_out:]
    grads_near = jnp.concatenate([grads_first, grads_second], axis=1)
    acts_near = acts_near.reshape(nb, na * act_blocks.shape[2], -1).astype(jnp.float32)
    grad_wide = gradient_held.astype(jnp.float32)
    eig_wide = eig_held.astype(jnp.float32)
    results = []
    for damping in range(dampings.shape[0]):
        precond = (grad_wide / (eig_wide + dampings[damping])).astype(jnp.bfloat16)
        projected = jnp.einsum("ij,sjt->sit", precond, grads_near, preferred_element_type=jnp.float32)
        results.append(jnp.sum(projected * acts_near, axis=1))
    partial = jnp.stack(results, axis=1)
    totals = partial[0]
    for shift in range(1, nb):
        totals = totals + lax.ppermute(partial[shift], "wb", perm=[(i, (i - shift) % nb) for i in range(nb)])
    query_count = query_act.shape[0] * lax.axis_size(WIDE)
    factor = mean_eig * (1.0 / math.sqrt(float(query_count) * eig_in * eig_out))
    train_weight = jnp.where(train_positions >= PROMPT, 1.0, 0.0).astype(jnp.float32)
    return totals * factor * train_weight[None, :]

def split_wide(size):
    wb = 1
    while wb * wb < size and size % (wb * 2) == 0:
        wb *= 2
    return size // wb, wb


def solution(mesh):
    groups, wide = mesh.devices.shape
    wa, wb = split_wide(wide)
    grid = Mesh(mesh.devices.reshape(groups, wa, wb), ("groups",) + WIDE)
    tokens = ("groups",) + WIDE
    in_specs = (
        P(tokens, None),
        P(tokens, None),
        P(tokens),
        P(None, WIDE),
        P(None, WIDE),
        P(WIDE, None),
        P("groups"),
        P(None, WIDE),
        P(None, WIDE),
        P(WIDE),
    )
    out_specs = P("groups", WIDE)
    return jax.shard_map(shards, mesh=grid, in_specs=in_specs, out_specs=out_specs, check_vma=False)
```

```python
import math

import jax
import jax.numpy as jnp
from jax import lax
from jax.sharding import Mesh
from jax.sharding import PartitionSpec as P

PROMPT = 1024
WIDE = ("wa", "wb")


def score_rows(grad_rows, eig_rows, dampings, train_act_rot, train_grad_rot):
    acts_rows = train_act_rot.astype(jnp.float32)
    grad_wide = grad_rows.astype(jnp.float32)
    eig_wide = eig_rows.astype(jnp.float32)
    results = []
    for damping in range(dampings.shape[0]):
        precond = (grad_wide / (eig_wide + dampings[damping])).astype(jnp.bfloat16)
        projected = jnp.dot(precond, train_grad_rot, preferred_element_type=jnp.float32)
        results.append(jnp.sum(projected * acts_rows, axis=0))
    return jnp.stack(results)


def ring_gather(x, axis):
    n = lax.axis_size(axis)
    parts = [x]
    for shift in range(1, n):
        parts.append(lax.ppermute(x, axis, perm=[(i, (i + shift) % n) for i in range(n)]))
    return jnp.stack(parts)


def natural_order(stacked, axis):
    n = stacked.shape[0]
    reverse = stacked[::-1]
    doubled = jnp.concatenate([reverse, reverse], axis=0)
    return lax.dynamic_slice_in_dim(doubled, n - 1 - lax.axis_index(axis), n, axis=0)


def shards(
    query_act,
    query_grad,
    query_positions,
    act_basis,
    grad_basis,
    eig_values,
    damping_index,
    train_act_rot,
    train_grad_rot,
    train_positions,
):
    nb = lax.axis_size("wb")
    na = lax.axis_size("wa")
    act_tokens = ring_gather(query_act, "wb")
    grad_tokens = ring_gather(query_grad, "wb")
    positions = ring_gather(query_positions, "wb")
    eig_sum = jnp.sum(eig_values.astype(jnp.float32))
    group_sum = eig_sum
    for shift in range(1, nb):
        group_sum = group_sum + lax.ppermute(eig_sum, "wb", perm=[(i, (i + shift) % nb) for i in range(nb)])
    act_tokens, grad_tokens, positions, group_sum = lax.optimization_barrier(
        (act_tokens, grad_tokens, positions, group_sum)
    )
    act_cols = lax.all_gather(act_basis, "wa", axis=1, tiled=True)
    grad_cols = lax.all_gather(grad_basis, "wa", axis=1, tiled=True)
    count = query_act.shape[0]
    act_rot = jnp.dot(
        act_tokens.reshape(nb * count, -1), act_cols, preferred_element_type=jnp.float32
    ).astype(jnp.bfloat16)
    grad_rot = jnp.dot(
        grad_tokens.reshape(nb * count, -1), grad_cols, preferred_element_type=jnp.float32
    ).astype(jnp.bfloat16)
    query_weight = jnp.where(positions.reshape(-1) >= PROMPT, 1.0, 0.0).astype(jnp.bfloat16)
    grad_kept = grad_rot * query_weight[:, None]
    act_rot = natural_order(act_rot.reshape(nb, count, -1), "wb").reshape(nb * count, -1)
    grad_kept = natural_order(grad_kept.reshape(nb, count, -1), "wb").reshape(nb * count, -1)
    grad_all = jnp.concatenate(list(ring_gather(grad_kept, "wb")), axis=1)
    partial_rows = lax.dot_general(
        act_rot, grad_all, (((0,), (0,)), ((), ())), preferred_element_type=jnp.float32
    )
    extra = jnp.broadcast_to(group_sum, (partial_rows.shape[0], 128))
    reduced = lax.psum_scatter(
        jnp.concatenate([partial_rows, extra], axis=1), "wa", scatter_dimension=0, tiled=True
    )
    rows = reduced.shape[0]
    by_shift = reduced[:, : partial_rows.shape[1]].reshape(rows, nb, na, -1).transpose(1, 0, 2, 3)
    gradient_rows = natural_order(by_shift, "wb").transpose(1, 2, 0, 3).reshape(rows, -1)
    me = lax.axis_index("wb")
    half = train_grad_rot.shape[0] // 2
    first_rows, train_act_rot, _ = lax.optimization_barrier((train_grad_rot[:half], train_act_rot, partial_rows))
    grads_first = ring_gather(first_rows, "wb")
    act_blocks = train_act_rot.reshape(na, nb, -1, train_act_rot.shape[1])
    acts_near = [act_blocks[:, me]]
    for shift in range(1, nb):
        outgoing = lax.dynamic_index_in_dim(act_blocks, (me + shift) % nb, axis=1, keepdims=False)
        acts_near.append(lax.ppermute(outgoing, "wb", perm=[(i, (i + shift) % nb) for i in range(nb)]))
    acts_near = jnp.stack(acts_near)
    eig_total = reduced[0, partial_rows.shape[1]]
    eig_in = eig_values.shape[0] * lax.axis_size(WIDE)
    eig_out = eig_values.shape[1]
    mean_eig = eig_total / (eig_in * eig_out)
    dampings = mean_eig * jnp.exp2(damping_index.astype(jnp.float32) - 4.0)
    payload = jnp.concatenate([gradient_rows.astype(jnp.bfloat16), eig_values], axis=1)
    grads_first, acts_near, payload = lax.optimization_barrier((grads_first, acts_near, payload))
    second_rows, _ = lax.optimization_barrier((train_grad_rot[half:], payload))
    grads_second = ring_gather(second_rows, "wb")
    rows_held = lax.all_gather(payload, "wa", axis=0, tiled=True)
    gradient_held, eig_held = rows_held[:, :eig_out], rows_held[:, eig_out:]
    grads_near = jnp.concatenate([grads_first, grads_second], axis=1)
    acts_near = acts_near.reshape(nb, na * act_blocks.shape[2], -1).astype(jnp.float32)
    grad_wide = gradient_held.astype(jnp.float32)
    eig_wide = eig_held.astype(jnp.float32)
    results = []
    for damping in range(dampings.shape[0]):
        precond = (grad_wide / (eig_wide + dampings[damping])).astype(jnp.bfloat16)
        projected = jnp.einsum("ij,sjt->sit", precond, grads_near, preferred_element_type=jnp.float32)
        results.append(jnp.sum(projected * acts_near, axis=1))
    partial = jnp.stack(results, axis=1)
    totals = partial[0]
    for shift in range(1, nb):
        totals = totals + lax.ppermute(partial[shift], "wb", perm=[(i, (i - shift) % nb) for i in range(nb)])
    query_count = query_act.shape[0] * lax.axis_size(WIDE)
    factor = mean_eig * (1.0 / math.sqrt(float(query_count) * eig_in * eig_out))
    train_weight = jnp.where(train_positions >= PROMPT, 1.0, 0.0).astype(jnp.float32)
    return totals * factor * train_weight[None, :]

def split_wide(size):
    wb = 1
    while wb * wb < size and size % (wb * 2) == 0:
        wb *= 2
    return size // wb, wb


def solution(mesh):
    groups, wide = mesh.devices.shape
    wa, wb = split_wide(wide)
    grid = Mesh(mesh.devices.reshape(groups, wa, wb), ("groups",) + WIDE)
    tokens = ("groups",) + WIDE
    in_specs = (
        P(tokens, None),
        P(tokens, None),
        P(tokens),
        P(None, WIDE),
        P(None, WIDE),
        P(WIDE, None),
        P("groups"),
        P(None, WIDE),
        P(None, WIDE),
        P(WIDE),
    )
    out_specs = P("groups", WIDE)
    return jax.shard_map(shards, mesh=grid, in_specs=in_specs, out_specs=out_specs, check_vma=False)
```

```python
import math

import jax
import jax.numpy as jnp
from jax import lax
from jax.sharding import Mesh
from jax.sharding import PartitionSpec as P

PROMPT = 1024
WIDE = ("wa", "wb")


def score_rows(grad_rows, eig_rows, dampings, train_act_rot, train_grad_rot):
    acts_rows = train_act_rot.astype(jnp.float32)
    grad_wide = grad_rows.astype(jnp.float32)
    eig_wide = eig_rows.astype(jnp.float32)
    results = []
    for damping in range(dampings.shape[0]):
        precond = (grad_wide / (eig_wide + dampings[damping])).astype(jnp.bfloat16)
        projected = jnp.dot(precond, train_grad_rot, preferred_element_type=jnp.float32)
        results.append(jnp.sum(projected * acts_rows, axis=0))
    return jnp.stack(results)


def ring_gather(x, axis):
    n = lax.axis_size(axis)
    parts = [x]
    for shift in range(1, n):
        parts.append(lax.ppermute(x, axis, perm=[(i, (i + shift) % n) for i in range(n)]))
    return jnp.stack(parts)


def natural_order(stacked, axis):
    n = stacked.shape[0]
    reverse = stacked[::-1]
    doubled = jnp.concatenate([reverse, reverse], axis=0)
    return lax.dynamic_slice_in_dim(doubled, n - 1 - lax.axis_index(axis), n, axis=0)


def shared_gather(rows):
    group_count = lax.axis_size("groups")
    size = rows.shape[0] // group_count
    mine = lax.dynamic_slice_in_dim(rows, lax.axis_index("groups") * size, size, axis=0)
    part = lax.all_gather(mine, "wa", axis=1, tiled=True)
    if group_count == 1:
        return part
    parts = natural_order(ring_gather(part, "groups"), "groups")
    return parts.reshape(group_count * size, -1)


def shards(
    query_act,
    query_grad,
    query_positions,
    act_basis,
    grad_basis,
    eig_values,
    damping_index,
    train_act_rot,
    train_grad_rot,
    train_positions,
):
    nb = lax.axis_size("wb")
    na = lax.axis_size("wa")
    act_tokens = ring_gather(query_act, "wb")
    grad_tokens = ring_gather(query_grad, "wb")
    positions = ring_gather(query_positions, "wb")
    eig_sum = jnp.sum(eig_values.astype(jnp.float32))
    group_sum = eig_sum
    for shift in range(1, nb):
        group_sum = group_sum + lax.ppermute(eig_sum, "wb", perm=[(i, (i + shift) % nb) for i in range(nb)])
    act_tokens, grad_tokens, positions, group_sum = lax.optimization_barrier(
        (act_tokens, grad_tokens, positions, group_sum)
    )
    act_cols = shared_gather(act_basis)
    depth = grad_basis.shape[0] // 2
    grad_cols = [shared_gather(grad_basis[:depth]), shared_gather(grad_basis[depth:])]
    count = query_act.shape[0]
    act_rot = jnp.dot(
        act_tokens.reshape(nb * count, -1), act_cols, preferred_element_type=jnp.float32
    ).astype(jnp.bfloat16)
    grad_flat = grad_tokens.reshape(nb * count, -1)
    grad_rot = (
        jnp.dot(grad_flat[:, :depth], grad_cols[0], preferred_element_type=jnp.float32)
        + jnp.dot(grad_flat[:, depth:], grad_cols[1], preferred_element_type=jnp.float32)
    ).astype(jnp.bfloat16)
    query_weight = jnp.where(positions.reshape(-1) >= PROMPT, 1.0, 0.0).astype(jnp.bfloat16)
    grad_kept = grad_rot * query_weight[:, None]
    act_rot = natural_order(act_rot.reshape(nb, count, -1), "wb").reshape(nb * count, -1)
    grad_kept = natural_order(grad_kept.reshape(nb, count, -1), "wb").reshape(nb * count, -1)
    grad_all = jnp.concatenate(list(ring_gather(grad_kept, "wb")), axis=1)
    partial_rows = lax.dot_general(
        act_rot, grad_all, (((0,), (0,)), ((), ())), preferred_element_type=jnp.float32
    )
    extra = jnp.broadcast_to(group_sum, (partial_rows.shape[0], 128))
    reduced = lax.psum_scatter(
        jnp.concatenate([partial_rows, extra], axis=1), "wa", scatter_dimension=0, tiled=True
    )
    rows = reduced.shape[0]
    by_shift = reduced[:, : partial_rows.shape[1]].reshape(rows, nb, na, -1).transpose(1, 0, 2, 3)
    gradient_rows = natural_order(by_shift, "wb").transpose(1, 2, 0, 3).reshape(rows, -1)
    me = lax.axis_index("wb")
    half = train_grad_rot.shape[0] // 2
    first_rows, train_act_rot, _ = lax.optimization_barrier((train_grad_rot[:half], train_act_rot, partial_rows))
    grads_first = ring_gather(first_rows, "wb")
    act_blocks = train_act_rot.reshape(na, nb, -1, train_act_rot.shape[1])
    acts_near = [act_blocks[:, me]]
    for shift in range(1, nb):
        outgoing = lax.dynamic_index_in_dim(act_blocks, (me + shift) % nb, axis=1, keepdims=False)
        acts_near.append(lax.ppermute(outgoing, "wb", perm=[(i, (i + shift) % nb) for i in range(nb)]))
    acts_near = jnp.stack(acts_near)
    eig_total = reduced[0, partial_rows.shape[1]]
    eig_in = eig_values.shape[0] * lax.axis_size(WIDE)
    eig_out = eig_values.shape[1]
    mean_eig = eig_total / (eig_in * eig_out)
    dampings = mean_eig * jnp.exp2(damping_index.astype(jnp.float32) - 4.0)
    payload = jnp.concatenate([gradient_rows.astype(jnp.bfloat16), eig_values], axis=1)
    grads_first, acts_near, payload = lax.optimization_barrier((grads_first, acts_near, payload))
    second_rows, _ = lax.optimization_barrier((train_grad_rot[half:], payload))
    grads_second = ring_gather(second_rows, "wb")
    rows_held = lax.all_gather(payload, "wa", axis=0, tiled=True)
    gradient_held, eig_held = rows_held[:, :eig_out], rows_held[:, eig_out:]
    grads_near = jnp.concatenate([grads_first, grads_second], axis=1)
    acts_near = acts_near.reshape(nb, na * act_blocks.shape[2], -1).astype(jnp.float32)
    grad_wide = gradient_held.astype(jnp.float32)
    eig_wide = eig_held.astype(jnp.float32)
    results = []
    for damping in range(dampings.shape[0]):
        precond = (grad_wide / (eig_wide + dampings[damping])).astype(jnp.bfloat16)
        projected = jnp.einsum("ij,sjt->sit", precond, grads_near, preferred_element_type=jnp.float32)
        results.append(jnp.sum(projected * acts_near, axis=1))
    partial = jnp.stack(results, axis=1)
    totals = partial[0]
    for shift in range(1, nb):
        totals = totals + lax.ppermute(partial[shift], "wb", perm=[(i, (i - shift) % nb) for i in range(nb)])
    query_count = query_act.shape[0] * lax.axis_size(WIDE)
    factor = mean_eig * (1.0 / math.sqrt(float(query_count) * eig_in * eig_out))
    train_weight = jnp.where(train_positions >= PROMPT, 1.0, 0.0).astype(jnp.float32)
    return totals * factor * train_weight[None, :]

def split_wide(size):
    wb = 1
    while wb * wb < size and size % (wb * 2) == 0:
        wb *= 2
    return size // wb, wb


def solution(mesh):
    groups, wide = mesh.devices.shape
    wa, wb = split_wide(wide)
    grid = Mesh(mesh.devices.reshape(groups, wa, wb), ("groups",) + WIDE)
    tokens = ("groups",) + WIDE
    in_specs = (
        P(tokens, None),
        P(tokens, None),
        P(tokens),
        P(None, WIDE),
        P(None, WIDE),
        P(WIDE, None),
        P("groups"),
        P(None, WIDE),
        P(None, WIDE),
        P(WIDE),
    )
    out_specs = P("groups", WIDE)
    return jax.shard_map(shards, mesh=grid, in_specs=in_specs, out_specs=out_specs, check_vma=False)
```

```python
import math

import jax
import jax.numpy as jnp
from jax import lax
from jax.sharding import Mesh
from jax.sharding import PartitionSpec as P

PROMPT = 1024
WIDE = ("wa", "wb")


def score_rows(grad_rows, eig_rows, dampings, train_act_rot, train_grad_rot):
    acts_rows = train_act_rot.astype(jnp.float32)
    grad_wide = grad_rows.astype(jnp.float32)
    eig_wide = eig_rows.astype(jnp.float32)
    results = []
    for damping in range(dampings.shape[0]):
        precond = (grad_wide / (eig_wide + dampings[damping])).astype(jnp.bfloat16)
        projected = jnp.dot(precond, train_grad_rot, preferred_element_type=jnp.float32)
        results.append(jnp.sum(projected * acts_rows, axis=0))
    return jnp.stack(results)


def ring_gather(x, axis):
    n = lax.axis_size(axis)
    parts = [x]
    for shift in range(1, n):
        parts.append(lax.ppermute(x, axis, perm=[(i, (i + shift) % n) for i in range(n)]))
    return jnp.stack(parts)


def natural_order(stacked, axis):
    n = stacked.shape[0]
    reverse = stacked[::-1]
    doubled = jnp.concatenate([reverse, reverse], axis=0)
    return lax.dynamic_slice_in_dim(doubled, n - 1 - lax.axis_index(axis), n, axis=0)


def shards(
    query_act,
    query_grad,
    query_positions,
    act_basis,
    grad_basis,
    eig_values,
    damping_index,
    train_act_rot,
    train_grad_rot,
    train_positions,
):
    nb = lax.axis_size("wb")
    na = lax.axis_size("wa")
    act_tokens = ring_gather(query_act, "wb")
    grad_tokens = ring_gather(query_grad, "wb")
    positions = ring_gather(query_positions, "wb")
    eig_sum = jnp.sum(eig_values.astype(jnp.float32))
    group_sum = eig_sum
    for shift in range(1, nb):
        group_sum = group_sum + lax.ppermute(eig_sum, "wb", perm=[(i, (i + shift) % nb) for i in range(nb)])
    eig_total = group_sum
    for shift in range(1, na):
        eig_total = eig_total + lax.ppermute(group_sum, "wa", perm=[(i, (i + shift) % na) for i in range(na)])
    act_tokens, grad_tokens, positions, eig_total = lax.optimization_barrier(
        (act_tokens, grad_tokens, positions, eig_total)
    )
    act_cols = lax.all_gather(act_basis, "wa", axis=1, tiled=True)
    grad_cols = lax.all_gather(grad_basis, "wa", axis=1, tiled=True)
    count = query_act.shape[0]
    act_rot = jnp.dot(
        act_tokens.reshape(nb * count, -1), act_cols, preferred_element_type=jnp.float32
    ).astype(jnp.bfloat16)
    grad_rot = jnp.dot(
        grad_tokens.reshape(nb * count, -1), grad_cols, preferred_element_type=jnp.float32
    ).astype(jnp.bfloat16)
    query_weight = jnp.where(positions.reshape(-1) >= PROMPT, 1.0, 0.0).astype(jnp.bfloat16)
    grad_kept = grad_rot * query_weight[:, None]
    act_rot = natural_order(act_rot.reshape(nb, count, -1), "wb").reshape(nb * count, -1)
    grad_kept = natural_order(grad_kept.reshape(nb, count, -1), "wb").reshape(nb * count, -1)
    grad_all = jnp.concatenate(list(ring_gather(grad_kept, "wb")), axis=1)
    partial_rows = lax.dot_general(
        act_rot, grad_all, (((0,), (0,)), ((), ())), preferred_element_type=jnp.float32
    )
    reduced = lax.psum_scatter(partial_rows.astype(jnp.bfloat16), "wa", scatter_dimension=0, tiled=True)
    rows = reduced.shape[0]
    by_shift = reduced.reshape(rows, nb, na, -1).transpose(1, 0, 2, 3)
    gradient_rows = natural_order(by_shift, "wb").transpose(1, 2, 0, 3).reshape(rows, -1)
    me = lax.axis_index("wb")
    half = train_grad_rot.shape[0] * 3 // 8
    first_rows, train_act_rot, _ = lax.optimization_barrier((train_grad_rot[:half], train_act_rot, partial_rows))
    grads_first = ring_gather(first_rows, "wb")
    act_blocks = train_act_rot.reshape(na, nb, -1, train_act_rot.shape[1])
    acts_near = [act_blocks[:, me]]
    for shift in range(1, nb):
        outgoing = lax.dynamic_index_in_dim(act_blocks, (me + shift) % nb, axis=1, keepdims=False)
        acts_near.append(lax.ppermute(outgoing, "wb", perm=[(i, (i + shift) % nb) for i in range(nb)]))
    acts_near = jnp.stack(acts_near)
    eig_in = eig_values.shape[0] * lax.axis_size(WIDE)
    eig_out = eig_values.shape[1]
    mean_eig = eig_total / (eig_in * eig_out)
    dampings = mean_eig * jnp.exp2(damping_index.astype(jnp.float32) - 4.0)
    payload = jnp.concatenate([gradient_rows.astype(jnp.bfloat16), eig_values], axis=1)
    grads_first, acts_near, payload = lax.optimization_barrier((grads_first, acts_near, payload))
    second_rows, _ = lax.optimization_barrier((train_grad_rot[half:], payload))
    grads_second = ring_gather(second_rows, "wb")
    rows_held = lax.all_gather(payload, "wa", axis=0, tiled=True)
    gradient_held, eig_held = rows_held[:, :eig_out], rows_held[:, eig_out:]
    grads_near = jnp.concatenate([grads_first, grads_second], axis=1)
    acts_near = acts_near.reshape(nb, na * act_blocks.shape[2], -1).astype(jnp.float32)
    grad_wide = gradient_held.astype(jnp.float32)
    eig_wide = eig_held.astype(jnp.float32)
    results = []
    for damping in range(dampings.shape[0]):
        precond = (grad_wide / (eig_wide + dampings[damping])).astype(jnp.bfloat16)
        projected = jnp.einsum("ij,sjt->sit", precond, grads_near, preferred_element_type=jnp.float32)
        results.append(jnp.sum(projected * acts_near, axis=1))
    partial = jnp.stack(results, axis=1)
    totals = partial[0]
    for shift in range(1, nb):
        totals = totals + lax.ppermute(partial[shift], "wb", perm=[(i, (i - shift) % nb) for i in range(nb)])
    query_count = query_act.shape[0] * lax.axis_size(WIDE)
    factor = mean_eig * (1.0 / math.sqrt(float(query_count) * eig_in * eig_out))
    train_weight = jnp.where(train_positions >= PROMPT, 1.0, 0.0).astype(jnp.float32)
    return totals * factor * train_weight[None, :]

def split_wide(size):
    wb = 1
    while wb * wb < size and size % (wb * 2) == 0:
        wb *= 2
    return size // wb, wb


def solution(mesh):
    groups, wide = mesh.devices.shape
    wa, wb = split_wide(wide)
    grid = Mesh(mesh.devices.reshape(groups, wa, wb), ("groups",) + WIDE)
    tokens = ("groups",) + WIDE
    in_specs = (
        P(tokens, None),
        P(tokens, None),
        P(tokens),
        P(None, WIDE),
        P(None, WIDE),
        P(WIDE, None),
        P("groups"),
        P(None, WIDE),
        P(None, WIDE),
        P(WIDE),
    )
    out_specs = P("groups", WIDE)
    return jax.shard_map(shards, mesh=grid, in_specs=in_specs, out_specs=out_specs, check_vma=False)
```

```python
import math

import jax
import jax.numpy as jnp
from jax import lax
from jax.sharding import Mesh
from jax.sharding import PartitionSpec as P

PROMPT = 1024
WIDE = ("wa", "wb")


def score_rows(grad_rows, eig_rows, dampings, train_act_rot, train_grad_rot):
    acts_rows = train_act_rot.astype(jnp.float32)
    grad_wide = grad_rows.astype(jnp.float32)
    eig_wide = eig_rows.astype(jnp.float32)
    results = []
    for damping in range(dampings.shape[0]):
        precond = (grad_wide / (eig_wide + dampings[damping])).astype(jnp.bfloat16)
        projected = jnp.dot(precond, train_grad_rot, preferred_element_type=jnp.float32)
        results.append(jnp.sum(projected * acts_rows, axis=0))
    return jnp.stack(results)


def ring_gather(x, axis):
    n = lax.axis_size(axis)
    parts = [x]
    for shift in range(1, n):
        parts.append(lax.ppermute(x, axis, perm=[(i, (i + shift) % n) for i in range(n)]))
    return jnp.stack(parts)


def natural_order(stacked, axis):
    n = stacked.shape[0]
    reverse = stacked[::-1]
    doubled = jnp.concatenate([reverse, reverse], axis=0)
    return lax.dynamic_slice_in_dim(doubled, n - 1 - lax.axis_index(axis), n, axis=0)


def shards(
    query_act,
    query_grad,
    query_positions,
    act_basis,
    grad_basis,
    eig_values,
    damping_index,
    train_act_rot,
    train_grad_rot,
    train_positions,
):
    nb = lax.axis_size("wb")
    na = lax.axis_size("wa")
    act_tokens = ring_gather(query_act, "wb")
    grad_tokens = ring_gather(query_grad, "wb")
    positions = ring_gather(query_positions, "wb")
    eig_sum = jnp.sum(eig_values.astype(jnp.float32))
    group_sum = eig_sum
    for shift in range(1, nb):
        group_sum = group_sum + lax.ppermute(eig_sum, "wb", perm=[(i, (i + shift) % nb) for i in range(nb)])
    act_tokens, grad_tokens, positions, group_sum = lax.optimization_barrier(
        (act_tokens, grad_tokens, positions, group_sum)
    )
    act_cols = lax.all_gather(act_basis, "wa", axis=1, tiled=True)
    grad_cols = lax.all_gather(grad_basis, "wa", axis=1, tiled=True)
    count = query_act.shape[0]
    eig_ready, _ = lax.optimization_barrier((eig_values, act_cols))
    eig_held = lax.all_gather(eig_ready, "wa", axis=0, tiled=True)
    act_rot = jnp.dot(
        act_tokens.reshape(nb * count, -1), act_cols, preferred_element_type=jnp.float32
    ).astype(jnp.bfloat16)
    grad_rot = jnp.dot(
        grad_tokens.reshape(nb * count, -1), grad_cols, preferred_element_type=jnp.float32
    ).astype(jnp.bfloat16)
    query_weight = jnp.where(positions.reshape(-1) >= PROMPT, 1.0, 0.0).astype(jnp.bfloat16)
    grad_kept = grad_rot * query_weight[:, None]
    act_rot = natural_order(act_rot.reshape(nb, count, -1), "wb").reshape(nb * count, -1)
    grad_kept = natural_order(grad_kept.reshape(nb, count, -1), "wb").reshape(nb * count, -1)
    grad_all = jnp.concatenate(list(ring_gather(grad_kept, "wb")), axis=1)
    partial_rows = lax.dot_general(
        act_rot, grad_all, (((0,), (0,)), ((), ())), preferred_element_type=jnp.float32
    )
    extra = jnp.broadcast_to(group_sum, (partial_rows.shape[0], 128))
    partial_rows, eig_held = lax.optimization_barrier((partial_rows, eig_held))
    reduced = lax.psum_scatter(
        jnp.concatenate([partial_rows, extra], axis=1), "wa", scatter_dimension=0, tiled=True
    )
    rows = reduced.shape[0]
    by_shift = reduced[:, : partial_rows.shape[1]].reshape(rows, nb, na, -1).transpose(1, 0, 2, 3)
    gradient_rows = natural_order(by_shift, "wb").transpose(1, 2, 0, 3).reshape(rows, -1)
    me = lax.axis_index("wb")
    half = train_grad_rot.shape[0] * 5 // 8
    first_rows, train_act_rot, _ = lax.optimization_barrier((train_grad_rot[:half], train_act_rot, partial_rows))
    grads_first = ring_gather(first_rows, "wb")
    act_blocks = train_act_rot.reshape(na, nb, -1, train_act_rot.shape[1])
    acts_near = [act_blocks[:, me]]
    for shift in range(1, nb):
        outgoing = lax.dynamic_index_in_dim(act_blocks, (me + shift) % nb, axis=1, keepdims=False)
        acts_near.append(lax.ppermute(outgoing, "wb", perm=[(i, (i + shift) % nb) for i in range(nb)]))
    acts_near = jnp.stack(acts_near)
    eig_total = reduced[0, partial_rows.shape[1]]
    eig_in = eig_values.shape[0] * lax.axis_size(WIDE)
    eig_out = eig_values.shape[1]
    mean_eig = eig_total / (eig_in * eig_out)
    dampings = mean_eig * jnp.exp2(damping_index.astype(jnp.float32) - 4.0)
    payload = gradient_rows.astype(jnp.bfloat16)
    grads_first, acts_near, payload = lax.optimization_barrier((grads_first, acts_near, payload))
    second_rows, _ = lax.optimization_barrier((train_grad_rot[half:], payload))
    grads_second = ring_gather(second_rows, "wb")
    gradient_held = lax.all_gather(payload, "wa", axis=0, tiled=True)
    grads_near = jnp.concatenate([grads_first, grads_second], axis=1)
    acts_near = acts_near.reshape(nb, na * act_blocks.shape[2], -1).astype(jnp.float32)
    grad_wide = gradient_held.astype(jnp.float32)
    eig_wide = eig_held.astype(jnp.float32)
    results = []
    for damping in range(dampings.shape[0]):
        precond = (grad_wide / (eig_wide + dampings[damping])).astype(jnp.bfloat16)
        projected = jnp.einsum("ij,sjt->sit", precond, grads_near, preferred_element_type=jnp.float32)
        results.append(jnp.sum(projected * acts_near, axis=1))
    partial = jnp.stack(results, axis=1)
    totals = partial[0]
    for shift in range(1, nb):
        totals = totals + lax.ppermute(partial[shift], "wb", perm=[(i, (i - shift) % nb) for i in range(nb)])
    query_count = query_act.shape[0] * lax.axis_size(WIDE)
    factor = mean_eig * (1.0 / math.sqrt(float(query_count) * eig_in * eig_out))
    train_weight = jnp.where(train_positions >= PROMPT, 1.0, 0.0).astype(jnp.float32)
    return totals * factor * train_weight[None, :]

def split_wide(size):
    wb = 1
    while wb * wb < size and size % (wb * 2) == 0:
        wb *= 2
    return size // wb, wb


def solution(mesh):
    groups, wide = mesh.devices.shape
    wa, wb = split_wide(wide)
    grid = Mesh(mesh.devices.reshape(groups, wa, wb), ("groups",) + WIDE)
    tokens = ("groups",) + WIDE
    in_specs = (
        P(tokens, None),
        P(tokens, None),
        P(tokens),
        P(None, WIDE),
        P(None, WIDE),
        P(WIDE, None),
        P("groups"),
        P(None, WIDE),
        P(None, WIDE),
        P(WIDE),
    )
    out_specs = P("groups", WIDE)
    return jax.shard_map(shards, mesh=grid, in_specs=in_specs, out_specs=out_specs, check_vma=False)
```

```python
import math

import jax
import jax.numpy as jnp
from jax import lax
from jax.sharding import Mesh
from jax.sharding import PartitionSpec as P

PROMPT = 1024
WIDE = ("wa", "wb")


def score_rows(grad_rows, eig_rows, dampings, train_act_rot, train_grad_rot):
    acts_rows = train_act_rot.astype(jnp.float32)
    grad_wide = grad_rows.astype(jnp.float32)
    eig_wide = eig_rows.astype(jnp.float32)
    results = []
    for damping in range(dampings.shape[0]):
        precond = (grad_wide / (eig_wide + dampings[damping])).astype(jnp.bfloat16)
        projected = jnp.dot(precond, train_grad_rot, preferred_element_type=jnp.float32)
        results.append(jnp.sum(projected * acts_rows, axis=0))
    return jnp.stack(results)


def ring_gather(x, axis):
    n = lax.axis_size(axis)
    parts = [x]
    for shift in range(1, n):
        parts.append(lax.ppermute(x, axis, perm=[(i, (i + shift) % n) for i in range(n)]))
    return jnp.stack(parts)


def natural_order(stacked, axis):
    n = stacked.shape[0]
    reverse = stacked[::-1]
    doubled = jnp.concatenate([reverse, reverse], axis=0)
    return lax.dynamic_slice_in_dim(doubled, n - 1 - lax.axis_index(axis), n, axis=0)


def rotate(x, start, axis):
    n = x.shape[axis]
    doubled = jnp.concatenate([x, x], axis=axis)
    return lax.dynamic_slice_in_dim(doubled, start, n, axis=axis)


def shards(
    query_act,
    query_grad,
    query_positions,
    act_basis,
    grad_basis,
    eig_values,
    damping_index,
    train_act_rot,
    train_grad_rot,
    train_positions,
):
    nb = lax.axis_size("wb")
    na = lax.axis_size("wa")
    act_tokens = ring_gather(query_act, "wb")
    grad_tokens = ring_gather(query_grad, "wb")
    positions = ring_gather(query_positions, "wb")
    act_tokens, grad_tokens, positions = lax.optimization_barrier((act_tokens, grad_tokens, positions))
    act_cols = lax.all_gather(act_basis, "wa", axis=1, tiled=True)
    grad_cols = lax.all_gather(grad_basis, "wa", axis=1, tiled=True)
    count = query_act.shape[0]
    act_rot = jnp.dot(
        act_tokens.reshape(nb * count, -1), act_cols, preferred_element_type=jnp.float32
    ).astype(jnp.bfloat16)
    grad_rot = jnp.dot(
        grad_tokens.reshape(nb * count, -1), grad_cols, preferred_element_type=jnp.float32
    ).astype(jnp.bfloat16)
    query_weight = jnp.where(positions.reshape(-1) >= PROMPT, 1.0, 0.0).astype(jnp.bfloat16)
    grad_kept = grad_rot * query_weight[:, None]
    act_rot = natural_order(act_rot.reshape(nb, count, -1), "wb").reshape(nb * count, -1)
    grad_kept = natural_order(grad_kept.reshape(nb, count, -1), "wb").reshape(nb * count, -1)
    grad_all = jnp.concatenate(list(ring_gather(grad_kept, "wb")), axis=1)
    partial_rows = lax.dot_general(
        act_rot, grad_all, (((0,), (0,)), ((), ())), preferred_element_type=jnp.float32
    )
    eig_sum = jnp.sum(eig_values.astype(jnp.float32))
    group_sum = eig_sum
    for shift in range(1, nb):
        group_sum = group_sum + lax.ppermute(eig_sum, "wb", perm=[(i, (i + shift) % nb) for i in range(nb)])
    extra = jnp.broadcast_to(group_sum, (partial_rows.shape[0], 128))
    reduced = lax.psum_scatter(
        jnp.concatenate([partial_rows, extra], axis=1), "wa", scatter_dimension=0, tiled=True
    )
    rows = reduced.shape[0]
    by_shift = reduced[:, : partial_rows.shape[1]].reshape(rows, nb, na, -1).transpose(1, 0, 2, 3)
    gradient_rows = natural_order(by_shift, "wb").transpose(1, 2, 0, 3).reshape(rows, -1)
    me = lax.axis_index("wb")
    half = train_grad_rot.shape[0] // 2
    first_rows, train_act_rot, _ = lax.optimization_barrier((train_grad_rot[:half], train_act_rot, partial_rows))
    grads_first = ring_gather(first_rows, "wb")
    act_blocks = train_act_rot.reshape(na, nb, -1, train_act_rot.shape[1])
    acts_near = [act_blocks[:, me]]
    for shift in range(1, nb):
        outgoing = lax.dynamic_index_in_dim(act_blocks, (me + shift) % nb, axis=1, keepdims=False)
        acts_near.append(lax.ppermute(outgoing, "wb", perm=[(i, (i + shift) % nb) for i in range(nb)]))
    acts_near = jnp.stack(acts_near)
    eig_total = reduced[0, partial_rows.shape[1]]
    eig_in = eig_values.shape[0] * lax.axis_size(WIDE)
    eig_out = eig_values.shape[1]
    mean_eig = eig_total / (eig_in * eig_out)
    dampings = mean_eig * jnp.exp2(damping_index.astype(jnp.float32) - 4.0)
    payload = jnp.concatenate([gradient_rows.astype(jnp.bfloat16), eig_values], axis=1)
    grads_first, acts_near, payload = lax.optimization_barrier((grads_first, acts_near, payload))
    second_rows, _ = lax.optimization_barrier((train_grad_rot[half:], payload))
    grads_second = ring_gather(second_rows, "wb")
    grads_near = jnp.concatenate([grads_first, grads_second], axis=1)
    acts_near = acts_near.astype(jnp.float32)

    def score_part(held, acts):
        grad_wide = held[:, :eig_out].astype(jnp.float32)
        eig_wide = held[:, eig_out:].astype(jnp.float32)
        results = []
        for damping in range(dampings.shape[0]):
            precond = (grad_wide / (eig_wide + dampings[damping])).astype(jnp.bfloat16)
            projected = jnp.einsum("ij,sjt->sit", precond, grads_near, preferred_element_type=jnp.float32)
            results.append(jnp.sum(projected * acts, axis=1))
        return jnp.stack(results, axis=1)

    mine = lax.axis_index("wa")
    own = score_part(payload, lax.dynamic_index_in_dim(acts_near, mine, axis=1, keepdims=False))
    rows_held = rotate(lax.all_gather(payload, "wa", axis=0), mine, 0)[1:]
    acts_rest = rotate(acts_near, mine, 1)[:, 1:]
    partial = own + score_part(
        rows_held.reshape(-1, rows_held.shape[-1]), acts_rest.reshape(nb, -1, acts_rest.shape[-1])
    )
    totals = partial[0]
    for shift in range(1, nb):
        totals = totals + lax.ppermute(partial[shift], "wb", perm=[(i, (i - shift) % nb) for i in range(nb)])
    query_count = query_act.shape[0] * lax.axis_size(WIDE)
    factor = mean_eig * (1.0 / math.sqrt(float(query_count) * eig_in * eig_out))
    train_weight = jnp.where(train_positions >= PROMPT, 1.0, 0.0).astype(jnp.float32)
    return totals * factor * train_weight[None, :]

def split_wide(size):
    wb = 1
    while wb * wb < size and size % (wb * 2) == 0:
        wb *= 2
    return size // wb, wb


def solution(mesh):
    groups, wide = mesh.devices.shape
    wa, wb = split_wide(wide)
    grid = Mesh(mesh.devices.reshape(groups, wa, wb), ("groups",) + WIDE)
    tokens = ("groups",) + WIDE
    in_specs = (
        P(tokens, None),
        P(tokens, None),
        P(tokens),
        P(None, WIDE),
        P(None, WIDE),
        P(WIDE, None),
        P("groups"),
        P(None, WIDE),
        P(None, WIDE),
        P(WIDE),
    )
    out_specs = P("groups", WIDE)
    return jax.shard_map(shards, mesh=grid, in_specs=in_specs, out_specs=out_specs, check_vma=False)
```

```python
import math

import jax
import jax.numpy as jnp
from jax import lax
from jax.sharding import Mesh
from jax.sharding import PartitionSpec as P

PROMPT = 1024
WIDE = ("wa", "wb")


def score_rows(grad_rows, eig_rows, dampings, train_act_rot, train_grad_rot):
    acts_rows = train_act_rot.astype(jnp.float32)
    grad_wide = grad_rows.astype(jnp.float32)
    eig_wide = eig_rows.astype(jnp.float32)
    results = []
    for damping in range(dampings.shape[0]):
        precond = (grad_wide / (eig_wide + dampings[damping])).astype(jnp.bfloat16)
        projected = jnp.dot(precond, train_grad_rot, preferred_element_type=jnp.float32)
        results.append(jnp.sum(projected * acts_rows, axis=0))
    return jnp.stack(results)


def ring_gather(x, axis):
    n = lax.axis_size(axis)
    parts = [x]
    for shift in range(1, n):
        parts.append(lax.ppermute(x, axis, perm=[(i, (i + shift) % n) for i in range(n)]))
    return jnp.stack(parts)


def natural_order(stacked, axis):
    n = stacked.shape[0]
    reverse = stacked[::-1]
    doubled = jnp.concatenate([reverse, reverse], axis=0)
    return lax.dynamic_slice_in_dim(doubled, n - 1 - lax.axis_index(axis), n, axis=0)


def rotate(x, start, axis):
    n = x.shape[axis]
    doubled = jnp.concatenate([x, x], axis=axis)
    return lax.dynamic_slice_in_dim(doubled, start, n, axis=axis)


def shards(
    query_act,
    query_grad,
    query_positions,
    act_basis,
    grad_basis,
    eig_values,
    damping_index,
    train_act_rot,
    train_grad_rot,
    train_positions,
):
    nb = lax.axis_size("wb")
    na = lax.axis_size("wa")
    act_tokens = ring_gather(query_act, "wb")
    grad_tokens = ring_gather(query_grad, "wb")
    positions = ring_gather(query_positions, "wb")
    act_tokens, grad_tokens, positions = lax.optimization_barrier((act_tokens, grad_tokens, positions))
    act_cols = lax.all_gather(act_basis, "wa", axis=1, tiled=True)
    grad_cols = lax.all_gather(grad_basis, "wa", axis=1, tiled=True)
    count = query_act.shape[0]
    act_rot = jnp.dot(
        act_tokens.reshape(nb * count, -1), act_cols, preferred_element_type=jnp.float32
    ).astype(jnp.bfloat16)
    grad_rot = jnp.dot(
        grad_tokens.reshape(nb * count, -1), grad_cols, preferred_element_type=jnp.float32
    ).astype(jnp.bfloat16)
    query_weight = jnp.where(positions.reshape(-1) >= PROMPT, 1.0, 0.0).astype(jnp.bfloat16)
    grad_kept = grad_rot * query_weight[:, None]
    act_rot = natural_order(act_rot.reshape(nb, count, -1), "wb").reshape(nb * count, -1)
    grad_kept = natural_order(grad_kept.reshape(nb, count, -1), "wb").reshape(nb * count, -1)
    grad_all = jnp.concatenate(list(ring_gather(grad_kept, "wb")), axis=1)
    partial_rows = lax.dot_general(
        act_rot, grad_all, (((0,), (0,)), ((), ())), preferred_element_type=jnp.float32
    )
    eig_sum = jnp.sum(eig_values.astype(jnp.float32))
    extra = jnp.broadcast_to(eig_sum, (partial_rows.shape[0], 128))
    reduced = lax.psum_scatter(
        jnp.concatenate([partial_rows, extra], axis=1), "wa", scatter_dimension=0, tiled=True
    )
    rows = reduced.shape[0]
    by_shift = reduced[:, : partial_rows.shape[1]].reshape(rows, nb, na, -1).transpose(1, 0, 2, 3)
    gradient_rows = natural_order(by_shift, "wb").transpose(1, 2, 0, 3).reshape(rows, -1)
    me = lax.axis_index("wb")
    half = train_grad_rot.shape[0] // 2
    first_rows, train_act_rot, _ = lax.optimization_barrier((train_grad_rot[:half], train_act_rot, partial_rows))
    grads_first = ring_gather(first_rows, "wb")
    act_blocks = train_act_rot.reshape(na, nb, -1, train_act_rot.shape[1])
    acts_near = [act_blocks[:, me]]
    for shift in range(1, nb):
        outgoing = lax.dynamic_index_in_dim(act_blocks, (me + shift) % nb, axis=1, keepdims=False)
        acts_near.append(lax.ppermute(outgoing, "wb", perm=[(i, (i + shift) % nb) for i in range(nb)]))
    acts_near = jnp.stack(acts_near)
    column_sum = reduced[0, partial_rows.shape[1]]
    eig_total = column_sum
    for shift in range(1, nb):
        eig_total = eig_total + lax.ppermute(column_sum, "wb", perm=[(i, (i + shift) % nb) for i in range(nb)])
    eig_in = eig_values.shape[0] * lax.axis_size(WIDE)
    eig_out = eig_values.shape[1]
    mean_eig = eig_total / (eig_in * eig_out)
    dampings = mean_eig * jnp.exp2(damping_index.astype(jnp.float32) - 4.0)
    payload = jnp.concatenate([gradient_rows.astype(jnp.bfloat16), eig_values], axis=1)
    grads_first, acts_near, payload = lax.optimization_barrier((grads_first, acts_near, payload))
    second_rows, _, eig_total = lax.optimization_barrier((train_grad_rot[half:], payload, eig_total))
    grads_second = ring_gather(second_rows, "wb")
    grads_near = jnp.concatenate([grads_first, grads_second], axis=1)
    acts_near = acts_near.astype(jnp.float32)

    def score_part(held, acts):
        grad_wide = held[:, :eig_out].astype(jnp.float32)
        eig_wide = held[:, eig_out:].astype(jnp.float32)
        results = []
        for damping in range(dampings.shape[0]):
            precond = (grad_wide / (eig_wide + dampings[damping])).astype(jnp.bfloat16)
            projected = jnp.einsum("ij,sjt->sit", precond, grads_near, preferred_element_type=jnp.float32)
            results.append(jnp.sum(projected * acts, axis=1))
        return jnp.stack(results, axis=1)

    mine = lax.axis_index("wa")
    own = score_part(payload, lax.dynamic_index_in_dim(acts_near, mine, axis=1, keepdims=False))
    rows_held = rotate(lax.all_gather(payload, "wa", axis=0), mine, 0)[1:]
    acts_rest = rotate(acts_near, mine, 1)[:, 1:]
    partial = own + score_part(
        rows_held.reshape(-1, rows_held.shape[-1]), acts_rest.reshape(nb, -1, acts_rest.shape[-1])
    )
    totals = partial[0]
    for shift in range(1, nb):
        totals = totals + lax.ppermute(partial[shift], "wb", perm=[(i, (i - shift) % nb) for i in range(nb)])
    query_count = query_act.shape[0] * lax.axis_size(WIDE)
    factor = mean_eig * (1.0 / math.sqrt(float(query_count) * eig_in * eig_out))
    train_weight = jnp.where(train_positions >= PROMPT, 1.0, 0.0).astype(jnp.float32)
    return totals * factor * train_weight[None, :]

def split_wide(size):
    wb = 1
    while wb * wb < size and size % (wb * 2) == 0:
        wb *= 2
    return size // wb, wb


def solution(mesh):
    groups, wide = mesh.devices.shape
    wa, wb = split_wide(wide)
    grid = Mesh(mesh.devices.reshape(groups, wa, wb), ("groups",) + WIDE)
    tokens = ("groups",) + WIDE
    in_specs = (
        P(tokens, None),
        P(tokens, None),
        P(tokens),
        P(None, WIDE),
        P(None, WIDE),
        P(WIDE, None),
        P("groups"),
        P(None, WIDE),
        P(None, WIDE),
        P(WIDE),
    )
    out_specs = P("groups", WIDE)
    return jax.shard_map(shards, mesh=grid, in_specs=in_specs, out_specs=out_specs, check_vma=False)
```

```python
import math

import jax
import jax.numpy as jnp
from jax import lax
from jax.sharding import Mesh
from jax.sharding import PartitionSpec as P

PROMPT = 1024
WIDE = ("wa", "wb")


def score_rows(grad_rows, eig_rows, dampings, train_act_rot, train_grad_rot):
    acts_rows = train_act_rot.astype(jnp.float32)
    grad_wide = grad_rows.astype(jnp.float32)
    eig_wide = eig_rows.astype(jnp.float32)
    results = []
    for damping in range(dampings.shape[0]):
        precond = (grad_wide / (eig_wide + dampings[damping])).astype(jnp.bfloat16)
        projected = jnp.dot(precond, train_grad_rot, preferred_element_type=jnp.float32)
        results.append(jnp.sum(projected * acts_rows, axis=0))
    return jnp.stack(results)


def ring_gather(x, axis):
    n = lax.axis_size(axis)
    parts = [x]
    for shift in range(1, n):
        parts.append(lax.ppermute(x, axis, perm=[(i, (i + shift) % n) for i in range(n)]))
    return jnp.stack(parts)


def natural_order(stacked, axis):
    n = stacked.shape[0]
    reverse = stacked[::-1]
    doubled = jnp.concatenate([reverse, reverse], axis=0)
    return lax.dynamic_slice_in_dim(doubled, n - 1 - lax.axis_index(axis), n, axis=0)


def rotate(x, start, axis):
    n = x.shape[axis]
    doubled = jnp.concatenate([x, x], axis=axis)
    return lax.dynamic_slice_in_dim(doubled, start, n, axis=axis)


def shards(
    query_act,
    query_grad,
    query_positions,
    act_basis,
    grad_basis,
    eig_values,
    damping_index,
    train_act_rot,
    train_grad_rot,
    train_positions,
):
    nb = lax.axis_size("wb")
    na = lax.axis_size("wa")
    act_tokens = ring_gather(query_act, "wb")
    grad_tokens = ring_gather(query_grad, "wb")
    positions = ring_gather(query_positions, "wb")
    act_tokens, grad_tokens, positions = lax.optimization_barrier((act_tokens, grad_tokens, positions))
    act_cols = lax.all_gather(act_basis, "wa", axis=1, tiled=True)
    grad_cols = lax.all_gather(grad_basis, "wa", axis=1, tiled=True)
    count = query_act.shape[0]
    act_rot = jnp.dot(
        act_tokens.reshape(nb * count, -1), act_cols, preferred_element_type=jnp.float32
    ).astype(jnp.bfloat16)
    grad_rot = jnp.dot(
        grad_tokens.reshape(nb * count, -1), grad_cols, preferred_element_type=jnp.float32
    ).astype(jnp.bfloat16)
    query_weight = jnp.where(positions.reshape(-1) >= PROMPT, 1.0, 0.0).astype(jnp.bfloat16)
    grad_kept = grad_rot * query_weight[:, None]
    act_rot = natural_order(act_rot.reshape(nb, count, -1), "wb").reshape(nb * count, -1)
    grad_kept = natural_order(grad_kept.reshape(nb, count, -1), "wb").reshape(nb * count, -1)
    grad_all = jnp.concatenate(list(ring_gather(grad_kept, "wb")), axis=1)
    partial_rows = lax.dot_general(
        act_rot, grad_all, (((0,), (0,)), ((), ())), preferred_element_type=jnp.float32
    )
    eig_sum = jnp.sum(eig_values.astype(jnp.float32))
    group_sum = eig_sum
    for shift in range(1, nb):
        group_sum = group_sum + lax.ppermute(eig_sum, "wb", perm=[(i, (i + shift) % nb) for i in range(nb)])
    extra = jnp.broadcast_to(group_sum, (partial_rows.shape[0], 128))
    reduced = lax.psum_scatter(
        jnp.concatenate([partial_rows, extra], axis=1), "wa", scatter_dimension=0, tiled=True
    )
    rows = reduced.shape[0]
    by_shift = reduced[:, : partial_rows.shape[1]].reshape(rows, nb, na, -1).transpose(1, 0, 2, 3)
    gradient_rows = natural_order(by_shift, "wb").transpose(1, 2, 0, 3).reshape(rows, -1)
    me = lax.axis_index("wb")
    half = train_grad_rot.shape[0] // 2
    first_rows, train_act_rot, _ = lax.optimization_barrier((train_grad_rot[:half], train_act_rot, partial_rows))
    grads_first = ring_gather(first_rows, "wb")
    act_blocks = train_act_rot.reshape(na, nb, -1, train_act_rot.shape[1])
    acts_near = [act_blocks[:, me]]
    for shift in range(1, nb):
        outgoing = lax.dynamic_index_in_dim(act_blocks, (me + shift) % nb, axis=1, keepdims=False)
        acts_near.append(lax.ppermute(outgoing, "wb", perm=[(i, (i + shift) % nb) for i in range(nb)]))
    acts_near = jnp.stack(acts_near)
    eig_total = reduced[0, partial_rows.shape[1]]
    eig_in = eig_values.shape[0] * lax.axis_size(WIDE)
    eig_out = eig_values.shape[1]
    mean_eig = eig_total / (eig_in * eig_out)
    dampings = mean_eig * jnp.exp2(damping_index.astype(jnp.float32) - 4.0)
    payload = jnp.concatenate([gradient_rows.astype(jnp.bfloat16), eig_values], axis=1)
    grads_first, acts_near, payload = lax.optimization_barrier((grads_first, acts_near, payload))
    second_rows, _ = lax.optimization_barrier((train_grad_rot[half:], payload))
    grads_second = ring_gather(second_rows, "wb")
    grads_near = jnp.concatenate([grads_first, grads_second], axis=1)
    grads_side = grads_near.transpose(1, 0, 2).reshape(grads_near.shape[1], -1)
    acts_near = acts_near.astype(jnp.float32)

    def score_part(held, acts):
        grad_wide = held[:, :eig_out].astype(jnp.float32)
        eig_wide = held[:, eig_out:].astype(jnp.float32)
        acts_side = acts.transpose(1, 0, 2).reshape(acts.shape[1], -1)
        results = []
        for damping in range(dampings.shape[0]):
            precond = (grad_wide / (eig_wide + dampings[damping])).astype(jnp.bfloat16)
            projected = jnp.dot(precond, grads_side, preferred_element_type=jnp.float32)
            results.append(jnp.sum(projected * acts_side, axis=0).reshape(nb, -1))
        return jnp.stack(results, axis=1)

    mine = lax.axis_index("wa")
    own = score_part(payload, lax.dynamic_index_in_dim(acts_near, mine, axis=1, keepdims=False))
    rows_held = rotate(lax.all_gather(payload, "wa", axis=0), mine, 0)[1:]
    acts_rest = rotate(acts_near, mine, 1)[:, 1:]
    partial = own + score_part(
        rows_held.reshape(-1, rows_held.shape[-1]), acts_rest.reshape(nb, -1, acts_rest.shape[-1])
    )
    totals = partial[0]
    for shift in range(1, nb):
        totals = totals + lax.ppermute(partial[shift], "wb", perm=[(i, (i - shift) % nb) for i in range(nb)])
    query_count = query_act.shape[0] * lax.axis_size(WIDE)
    factor = mean_eig * (1.0 / math.sqrt(float(query_count) * eig_in * eig_out))
    train_weight = jnp.where(train_positions >= PROMPT, 1.0, 0.0).astype(jnp.float32)
    return totals * factor * train_weight[None, :]

def split_wide(size):
    wb = 1
    while wb * wb < size and size % (wb * 2) == 0:
        wb *= 2
    return size // wb, wb


def solution(mesh):
    groups, wide = mesh.devices.shape
    wa, wb = split_wide(wide)
    grid = Mesh(mesh.devices.reshape(groups, wa, wb), ("groups",) + WIDE)
    tokens = ("groups",) + WIDE
    in_specs = (
        P(tokens, None),
        P(tokens, None),
        P(tokens),
        P(None, WIDE),
        P(None, WIDE),
        P(WIDE, None),
        P("groups"),
        P(None, WIDE),
        P(None, WIDE),
        P(WIDE),
    )
    out_specs = P("groups", WIDE)
    return jax.shard_map(shards, mesh=grid, in_specs=in_specs, out_specs=out_specs, check_vma=False)
```

```python
import math

import jax
import jax.numpy as jnp
from jax import lax
from jax.sharding import Mesh
from jax.sharding import PartitionSpec as P

PROMPT = 1024
WIDE = ("wa", "wb")


def score_rows(grad_rows, eig_rows, dampings, train_act_rot, train_grad_rot):
    acts_rows = train_act_rot.astype(jnp.float32)
    grad_wide = grad_rows.astype(jnp.float32)
    eig_wide = eig_rows.astype(jnp.float32)
    results = []
    for damping in range(dampings.shape[0]):
        precond = (grad_wide / (eig_wide + dampings[damping])).astype(jnp.bfloat16)
        projected = jnp.dot(precond, train_grad_rot, preferred_element_type=jnp.float32)
        results.append(jnp.sum(projected * acts_rows, axis=0))
    return jnp.stack(results)


def ring_gather(x, axis):
    n = lax.axis_size(axis)
    parts = [x]
    for shift in range(1, n):
        parts.append(lax.ppermute(x, axis, perm=[(i, (i + shift) % n) for i in range(n)]))
    return jnp.stack(parts)


def natural_order(stacked, axis):
    n = stacked.shape[0]
    reverse = stacked[::-1]
    doubled = jnp.concatenate([reverse, reverse], axis=0)
    return lax.dynamic_slice_in_dim(doubled, n - 1 - lax.axis_index(axis), n, axis=0)


def rotate(x, start, axis):
    n = x.shape[axis]
    doubled = jnp.concatenate([x, x], axis=axis)
    return lax.dynamic_slice_in_dim(doubled, start, n, axis=axis)


def shards(
    query_act,
    query_grad,
    query_positions,
    act_basis,
    grad_basis,
    eig_values,
    damping_index,
    train_act_rot,
    train_grad_rot,
    train_positions,
):
    nb = lax.axis_size("wb")
    na = lax.axis_size("wa")
    act_tokens = ring_gather(query_act, "wb")
    grad_tokens = ring_gather(query_grad, "wb")
    positions = ring_gather(query_positions, "wb")
    act_tokens, grad_tokens, positions = lax.optimization_barrier((act_tokens, grad_tokens, positions))
    act_cols = lax.all_gather(act_basis, "wa", axis=1, tiled=True)
    width = grad_basis.shape[1] // 2
    grad_cols = [
        lax.all_gather(grad_basis[:, :width], "wa", axis=1, tiled=True),
        lax.all_gather(grad_basis[:, width:], "wa", axis=1, tiled=True),
    ]
    count = query_act.shape[0]
    act_rot = jnp.dot(
        act_tokens.reshape(nb * count, -1), act_cols, preferred_element_type=jnp.float32
    ).astype(jnp.bfloat16)
    query_weight = jnp.where(positions.reshape(-1) >= PROMPT, 1.0, 0.0).astype(jnp.bfloat16)
    act_rot = natural_order(act_rot.reshape(nb, count, -1), "wb").reshape(nb * count, -1)
    partials = []
    for cols in grad_cols:
        grad_rot = jnp.dot(
            grad_tokens.reshape(nb * count, -1), cols, preferred_element_type=jnp.float32
        ).astype(jnp.bfloat16)
        grad_kept = grad_rot * query_weight[:, None]
        grad_kept = natural_order(grad_kept.reshape(nb, count, -1), "wb").reshape(nb * count, -1)
        grad_all = jnp.concatenate(list(ring_gather(grad_kept, "wb")), axis=1)
        partials.append(lax.dot_general(
            act_rot, grad_all, (((0,), (0,)), ((), ())), preferred_element_type=jnp.float32
        ))
    partial_rows = jnp.concatenate(partials, axis=1)
    eig_sum = jnp.sum(eig_values.astype(jnp.float32))
    group_sum = eig_sum
    for shift in range(1, nb):
        group_sum = group_sum + lax.ppermute(eig_sum, "wb", perm=[(i, (i + shift) % nb) for i in range(nb)])
    extra = jnp.broadcast_to(group_sum, (partial_rows.shape[0], 128))
    reduced = lax.psum_scatter(
        jnp.concatenate([partial_rows, extra], axis=1), "wa", scatter_dimension=0, tiled=True
    )
    rows = reduced.shape[0]
    by_shift = reduced[:, : partial_rows.shape[1]].reshape(rows, 2, nb, na, -1).transpose(2, 0, 1, 3, 4)
    gradient_rows = natural_order(by_shift, "wb").transpose(1, 3, 0, 2, 4).reshape(rows, -1)
    me = lax.axis_index("wb")
    half = train_grad_rot.shape[0] // 2
    first_rows, train_act_rot, _ = lax.optimization_barrier((train_grad_rot[:half], train_act_rot, partial_rows))
    grads_first = ring_gather(first_rows, "wb")
    act_blocks = train_act_rot.reshape(na, nb, -1, train_act_rot.shape[1])
    acts_near = [act_blocks[:, me]]
    for shift in range(1, nb):
        outgoing = lax.dynamic_index_in_dim(act_blocks, (me + shift) % nb, axis=1, keepdims=False)
        acts_near.append(lax.ppermute(outgoing, "wb", perm=[(i, (i + shift) % nb) for i in range(nb)]))
    acts_near = jnp.stack(acts_near)
    eig_total = reduced[0, partial_rows.shape[1]]
    eig_in = eig_values.shape[0] * lax.axis_size(WIDE)
    eig_out = eig_values.shape[1]
    mean_eig = eig_total / (eig_in * eig_out)
    dampings = mean_eig * jnp.exp2(damping_index.astype(jnp.float32) - 4.0)
    payload = jnp.concatenate([gradient_rows.astype(jnp.bfloat16), eig_values], axis=1)
    grads_first, acts_near, payload = lax.optimization_barrier((grads_first, acts_near, payload))
    second_rows, _ = lax.optimization_barrier((train_grad_rot[half:], payload))
    grads_second = ring_gather(second_rows, "wb")
    grads_near = jnp.concatenate([grads_first, grads_second], axis=1)
    acts_near = acts_near.astype(jnp.float32)

    def score_part(held, acts):
        grad_wide = held[:, :eig_out].astype(jnp.float32)
        eig_wide = held[:, eig_out:].astype(jnp.float32)
        results = []
        for damping in range(dampings.shape[0]):
            precond = (grad_wide / (eig_wide + dampings[damping])).astype(jnp.bfloat16)
            projected = jnp.einsum("ij,sjt->sit", precond, grads_near, preferred_element_type=jnp.float32)
            results.append(jnp.sum(projected * acts, axis=1))
        return jnp.stack(results, axis=1)

    mine = lax.axis_index("wa")
    own = score_part(payload, lax.dynamic_index_in_dim(acts_near, mine, axis=1, keepdims=False))
    rows_held = rotate(lax.all_gather(payload, "wa", axis=0), mine, 0)[1:]
    acts_rest = rotate(acts_near, mine, 1)[:, 1:]
    partial = own + score_part(
        rows_held.reshape(-1, rows_held.shape[-1]), acts_rest.reshape(nb, -1, acts_rest.shape[-1])
    )
    totals = partial[0]
    for shift in range(1, nb):
        totals = totals + lax.ppermute(partial[shift], "wb", perm=[(i, (i - shift) % nb) for i in range(nb)])
    query_count = query_act.shape[0] * lax.axis_size(WIDE)
    factor = mean_eig * (1.0 / math.sqrt(float(query_count) * eig_in * eig_out))
    train_weight = jnp.where(train_positions >= PROMPT, 1.0, 0.0).astype(jnp.float32)
    return totals * factor * train_weight[None, :]

def split_wide(size):
    wb = 1
    while wb * wb < size and size % (wb * 2) == 0:
        wb *= 2
    return size // wb, wb


def solution(mesh):
    groups, wide = mesh.devices.shape
    wa, wb = split_wide(wide)
    grid = Mesh(mesh.devices.reshape(groups, wa, wb), ("groups",) + WIDE)
    tokens = ("groups",) + WIDE
    in_specs = (
        P(tokens, None),
        P(tokens, None),
        P(tokens),
        P(None, WIDE),
        P(None, WIDE),
        P(WIDE, None),
        P("groups"),
        P(None, WIDE),
        P(None, WIDE),
        P(WIDE),
    )
    out_specs = P("groups", WIDE)
    return jax.shard_map(shards, mesh=grid, in_specs=in_specs, out_specs=out_specs, check_vma=False)
```

```python
import math

import jax
import jax.numpy as jnp
from jax import lax
from jax.sharding import Mesh
from jax.sharding import PartitionSpec as P

PROMPT = 1024
WIDE = ("wa", "wb")


def score_rows(grad_rows, eig_rows, dampings, train_act_rot, train_grad_rot):
    acts_rows = train_act_rot.astype(jnp.float32)
    grad_wide = grad_rows.astype(jnp.float32)
    eig_wide = eig_rows.astype(jnp.float32)
    results = []
    for damping in range(dampings.shape[0]):
        precond = (grad_wide / (eig_wide + dampings[damping])).astype(jnp.bfloat16)
        projected = jnp.dot(precond, train_grad_rot, preferred_element_type=jnp.float32)
        results.append(jnp.sum(projected * acts_rows, axis=0))
    return jnp.stack(results)


def ring_gather(x, axis):
    n = lax.axis_size(axis)
    parts = [x]
    for shift in range(1, n):
        parts.append(lax.ppermute(x, axis, perm=[(i, (i + shift) % n) for i in range(n)]))
    return jnp.stack(parts)


def natural_order(stacked, axis):
    n = stacked.shape[0]
    reverse = stacked[::-1]
    doubled = jnp.concatenate([reverse, reverse], axis=0)
    return lax.dynamic_slice_in_dim(doubled, n - 1 - lax.axis_index(axis), n, axis=0)


def rotate(x, start, axis):
    n = x.shape[axis]
    doubled = jnp.concatenate([x, x], axis=axis)
    return lax.dynamic_slice_in_dim(doubled, start, n, axis=axis)


def shards(
    query_act,
    query_grad,
    query_positions,
    act_basis,
    grad_basis,
    eig_values,
    damping_index,
    train_act_rot,
    train_grad_rot,
    train_positions,
):
    nb = lax.axis_size("wb")
    na = lax.axis_size("wa")
    act_tokens = ring_gather(query_act, "wb")
    grad_tokens = ring_gather(query_grad, "wb")
    positions = ring_gather(query_positions, "wb")
    act_tokens, grad_tokens, positions = lax.optimization_barrier((act_tokens, grad_tokens, positions))
    act_cols = lax.all_gather(act_basis, "wa", axis=1, tiled=True)
    grad_cols = lax.all_gather(grad_basis, "wa", axis=1, tiled=True)
    count = query_act.shape[0]
    act_rot = jnp.dot(
        act_tokens.reshape(nb * count, -1), act_cols, preferred_element_type=jnp.float32
    ).astype(jnp.bfloat16)
    grad_rot = jnp.dot(
        grad_tokens.reshape(nb * count, -1), grad_cols, preferred_element_type=jnp.float32
    ).astype(jnp.bfloat16)
    query_weight = jnp.where(positions.reshape(-1) >= PROMPT, 1.0, 0.0).astype(jnp.bfloat16)
    grad_kept = grad_rot * query_weight[:, None]
    act_rot = natural_order(act_rot.reshape(nb, count, -1), "wb").reshape(nb * count, -1)
    grad_kept = natural_order(grad_kept.reshape(nb, count, -1), "wb").reshape(nb * count, -1)
    grad_all = jnp.concatenate(list(ring_gather(grad_kept, "wb")), axis=1)
    partial_rows = lax.dot_general(
        act_rot, grad_all, (((0,), (0,)), ((), ())), preferred_element_type=jnp.float32
    )
    eig_sum = jnp.sum(eig_values.astype(jnp.float32))
    group_sum = eig_sum
    for shift in range(1, nb):
        group_sum = group_sum + lax.ppermute(eig_sum, "wb", perm=[(i, (i + shift) % nb) for i in range(nb)])
    extra = jnp.broadcast_to(group_sum, (partial_rows.shape[0], 128))
    reduced = lax.psum_scatter(
        jnp.concatenate([partial_rows, extra], axis=1), "wa", scatter_dimension=0, tiled=True
    )
    rows = reduced.shape[0]
    by_shift = reduced[:, : partial_rows.shape[1]].astype(jnp.bfloat16).reshape(rows, nb, na, -1).transpose(1, 0, 2, 3)
    gradient_rows = natural_order(by_shift, "wb").transpose(1, 2, 0, 3).reshape(rows, -1)
    me = lax.axis_index("wb")
    half = train_grad_rot.shape[0] // 2
    first_rows, train_act_rot, _ = lax.optimization_barrier((train_grad_rot[:half], train_act_rot, partial_rows))
    grads_first = ring_gather(first_rows, "wb")
    act_blocks = train_act_rot.reshape(na, nb, -1, train_act_rot.shape[1])
    acts_near = [act_blocks[:, me]]
    for shift in range(1, nb):
        outgoing = lax.dynamic_index_in_dim(act_blocks, (me + shift) % nb, axis=1, keepdims=False)
        acts_near.append(lax.ppermute(outgoing, "wb", perm=[(i, (i + shift) % nb) for i in range(nb)]))
    acts_near = jnp.stack(acts_near)
    eig_total = reduced[0, partial_rows.shape[1]]
    eig_in = eig_values.shape[0] * lax.axis_size(WIDE)
    eig_out = eig_values.shape[1]
    mean_eig = eig_total / (eig_in * eig_out)
    dampings = mean_eig * jnp.exp2(damping_index.astype(jnp.float32) - 4.0)
    payload = jnp.concatenate([gradient_rows, eig_values], axis=1)
    grads_first, acts_near, payload = lax.optimization_barrier((grads_first, acts_near, payload))
    second_rows, _ = lax.optimization_barrier((train_grad_rot[half:], payload))
    grads_second = ring_gather(second_rows, "wb")
    grads_near = jnp.concatenate([grads_first, grads_second], axis=1)
    acts_near = acts_near.astype(jnp.float32)

    def score_part(held, acts):
        grad_wide = held[:, :eig_out].astype(jnp.float32)
        eig_wide = held[:, eig_out:].astype(jnp.float32)
        results = []
        for damping in range(dampings.shape[0]):
            precond = (grad_wide / (eig_wide + dampings[damping])).astype(jnp.bfloat16)
            projected = jnp.einsum("ij,sjt->sit", precond, grads_near, preferred_element_type=jnp.float32)
            results.append(jnp.sum(projected * acts, axis=1))
        return jnp.stack(results, axis=1)

    mine = lax.axis_index("wa")
    own = score_part(payload, lax.dynamic_index_in_dim(acts_near, mine, axis=1, keepdims=False))
    rows_held = rotate(lax.all_gather(payload, "wa", axis=0), mine, 0)[1:]
    acts_rest = rotate(acts_near, mine, 1)[:, 1:]
    partial = own + score_part(
        rows_held.reshape(-1, rows_held.shape[-1]), acts_rest.reshape(nb, -1, acts_rest.shape[-1])
    )
    totals = partial[0]
    for shift in range(1, nb):
        totals = totals + lax.ppermute(partial[shift], "wb", perm=[(i, (i - shift) % nb) for i in range(nb)])
    query_count = query_act.shape[0] * lax.axis_size(WIDE)
    factor = mean_eig * (1.0 / math.sqrt(float(query_count) * eig_in * eig_out))
    train_weight = jnp.where(train_positions >= PROMPT, 1.0, 0.0).astype(jnp.float32)
    return totals * factor * train_weight[None, :]

def split_wide(size):
    wb = 1
    while wb * wb < size and size % (wb * 2) == 0:
        wb *= 2
    return size // wb, wb


def solution(mesh):
    groups, wide = mesh.devices.shape
    wa, wb = split_wide(wide)
    grid = Mesh(mesh.devices.reshape(groups, wa, wb), ("groups",) + WIDE)
    tokens = ("groups",) + WIDE
    in_specs = (
        P(tokens, None),
        P(tokens, None),
        P(tokens),
        P(None, WIDE),
        P(None, WIDE),
        P(WIDE, None),
        P("groups"),
        P(None, WIDE),
        P(None, WIDE),
        P(WIDE),
    )
    out_specs = P("groups", WIDE)
    return jax.shard_map(shards, mesh=grid, in_specs=in_specs, out_specs=out_specs, check_vma=False)
```
